128 devices in a mesh: section: 4 (over z), fsdp: 32 (over x, y, core).
Axes of the slice: x: 4, y: 4, z: 4, core: 2. Of those that a mesh axis runs over, the one named last changes fastest.
Arguments:
- saved_inputs: bfloat16 [4, 4, 1536, 2048], P('section', None, 'fsdp'), may hold values from -6 to 6
- attn_weights: bfloat16 [4, 2048, 4096], P('section', 'fsdp'), may hold values from -16 to 16
- grad_out: bfloat16 [4, 1536, 2048], P(None, 'fsdp'), may hold values from -1.1953125 to 1.1953125
- segments: int32 [4, 32, 48], P(None, 'fsdp'), may hold values from 0 to 2, never falling along the last dimension, each value on 1 to 24 neighbouring positions
- coords: float32 [3, 4, 1536], P(None, None, 'fsdp'), may hold values from -4 to 4
- embed_in: bfloat16 [2048, 4], P(('section', 'fsdp')), may hold values from -4 to 4
- embed_out: bfloat16 [2048, 2048], P(('section', 'fsdp')), may hold values from -0.125 to 0.125
Outputs:
- attn_grad: float32 [4, 2048, 4096], P('section', 'fsdp')
- input_grad: bfloat16 [4, 1536, 2048], P(None, 'fsdp')
- embed_out_grad: float32 [2048, 2048], P(('section', 'fsdp'))
- embed_in_grad: float32 [2048, 4], P(('section', 'fsdp'))
The draws below stay inside these ranges and needn't reach their ends.
Inputs may be any that keep to these rules, and one draw needn't show every extreme that they name: `segments`: sessions never straddle a block of 48 tokens; within a block segment numbers never fall and each session is one run of at most 24 tokens.
All inputs are finite; a program needn't handle non-finite values.
Results may differ from the reference program's by a relative error of at most 0.02.
Values may be sent and summed in bfloat16 or wider, within the bound.
No kernel may reach another device: no remote copies, remote signals or barrier semaphores. Data moves between devices by JAX's collectives and lax.ppermute only.
A program may use at most 128 MiB of HBM per device.

```python
import math
import jax
import jax.numpy as jnp
import numpy as np
from jax import lax

D = 2048
HEADS = 16
HEAD_DIM = 64
HID = 2048
ROWS = 48
MICRO = 4
SESS = 3
AW = 1024
LAYERS = 4
BLOCKS = 32
TOKENS = 1536
N_FSDP = 32


def draw_attn_weights(key, part):
    attn_width = HEADS * HEAD_DIM
    shape = (LAYERS, D, 4 * attn_width)
    first_key = jax.random.fold_in(key, 11)
    base = jax.random.normal(first_key, shape, jnp.float32)
    column = jnp.arange(4 * attn_width)
    fan = jnp.where(column < 3 * attn_width, D, attn_width).astype(jnp.float32)
    weights = base / jnp.sqrt(fan)[None, None, :]
    return weights.astype(jnp.bfloat16)


def level_of(rng, shape, split, low, top_value):
    factor_of = 1.0
    for position, blocks in split:
        steps = jax.random.uniform(jax.random.fold_in(jax.random.fold_in(rng, 6), position), (blocks,), jnp.float32, low / len(split), top_value / len(split))
        factor_of = factor_of * jnp.repeat(jnp.exp(steps), shape[position] // blocks).reshape((-1,) + (1,) * (len(shape) - 1 - position))
    return factor_of


def length_profile(amount, total, bound, skew):
    weights = [(1 << 20) // math.isqrt(rank ** skew) + 1 for rank in range(2, amount + 1)]
    spare, counts = total - bound - (amount - 1), [1] * (amount - 1)
    while spare > 0:
        candidates = [i for i in range(amount - 1) if counts[i] < bound]
        whole, remaining = sum([weights[i] for i in candidates]), spare
        for i in candidates:
            addition = min(bound - counts[i], max(1, remaining * weights[i] // whole), spare)
            counts[i] = counts[i] + addition
            spare = spare - addition
    return np.array([bound] + counts)


def uneven(stream_key, number_of, total, bound, slope):
    if number_of == 2:
        one = jax.random.randint(stream_key, (), max(1, total - bound), min(bound, total - 1) + 1)
        return jnp.stack([one, total - one])
    sizes = jnp.asarray(length_profile(number_of, total, bound, slope), jnp.int32)
    couples = (number_of - 1) // 2
    donor, taker = sizes[1:1 + 2 * couples:2], sizes[2:2 + 2 * couples:2]
    margin = jnp.minimum(donor - 1, bound - taker)
    moved = jax.random.randint(jax.random.fold_in(stream_key, 1), (couples,), 0, 1 << 20) % (margin + 1)
    sizes = sizes.at[1:1 + 2 * couples:2].set(donor - moved).at[2:2 + 2 * couples:2].set(taker + moved)
    return sizes[jax.random.permutation(jax.random.fold_in(stream_key, 2), number_of)]


def normal_values(key, shape, width, reach, shards=(), held_as=jnp.bfloat16):
    values = width * jax.random.normal(key, shape, jnp.float32)
    if shards:
        values = values * level_of(key, shape, shards, -0.22, 0.18)
    return jnp.clip(values, -reach, reach).astype(held_as)


def setup_inputs(seed: int = 0) -> dict:
    key_of = jax.random.split(jax.random.key(seed), 8)
    saved_inputs = normal_values(key_of[0], (LAYERS, MICRO, TOKENS, D), 1.0, 6.0, ((0, 4), (2, 32)))
    attn_weights = draw_attn_weights(jax.random.fold_in(key_of[7], 71), 0)
    grad_out = normal_values(key_of[2], (MICRO, TOKENS, D), 0.2, 1.1953125, ((1, 32),))
    segments = jax.vmap(lambda own: jnp.searchsorted(jnp.cumsum(uneven(own, SESS, ROWS, ROWS // 2, 0)), jnp.arange(ROWS), side="right"))(jax.random.split(key_of[3], MICRO * BLOCKS)).reshape((MICRO, BLOCKS, ROWS)).astype(jnp.int32)
    coords = normal_values(key_of[4], (3, MICRO, TOKENS), 1.0, 4.0, ((2, 32),), jnp.float32)
    embed_in = normal_values(key_of[5], (HID, 4), 1.0, 4.0, ((0, 128),))
    embed_out = normal_values(key_of[6], (HID, D), HID ** -0.5, 0.125, ((0, 128),))
    return {"saved_inputs": saved_inputs, "attn_weights": attn_weights, "grad_out": grad_out, "segments": segments, "coords": coords, "embed_in": embed_in, "embed_out": embed_out}


EPS = 1e-05

def gelu_value(pre):
    return 0.5 * pre * (1.0 + jax.scipy.special.erf(pre / jnp.sqrt(2.0)))

def gelu_slope(pre):
    return 0.5 * (1.0 + jax.scipy.special.erf(pre / jnp.sqrt(2.0))) + pre * jnp.exp(-0.5 * pre * pre) / jnp.sqrt(2.0 * jnp.pi)

def layer_backward(inputs, upstream, segment, weights):
    row_count = inputs.shape[0]
    attn_width = weights.shape[1] // 4
    head_count = attn_width // HEAD_DIM
    scaling = HEAD_DIM ** (-0.5)
    values = inputs.astype(jnp.float32)
    norm_scale = lax.rsqrt(lax.optimization_barrier(jnp.mean(values * values, axis=-1, keepdims=True)) + EPS)
    normed = (values * norm_scale).astype(jnp.bfloat16)
    projection = weights[:, :3 * attn_width]
    projected = jnp.dot(normed, projection, preferred_element_type=jnp.float32).astype(jnp.bfloat16)
    queries = projected[:, :attn_width].reshape(row_count, head_count, HEAD_DIM).astype(jnp.float32)
    key_rows = projected[:, attn_width:2 * attn_width].reshape(row_count, head_count, HEAD_DIM).astype(jnp.float32)
    value_rows = projected[:, 2 * attn_width:].reshape(row_count, head_count, HEAD_DIM).astype(jnp.float32)
    scores = jnp.einsum('qhd,khd->hqk', queries, key_rows) * scaling
    same_session = segment[:, None] == segment[None, :]
    scores = jnp.where(same_session[None], scores, -1e+30)
    row_peak = lax.optimization_barrier(jnp.max(scores, axis=-1, keepdims=True))
    exponent = jnp.exp(scores - row_peak)
    probabilities = exponent / lax.optimization_barrier(jnp.sum(exponent, axis=-1, keepdims=True))
    prob_rounded = probabilities.astype(jnp.bfloat16).astype(jnp.float32)
    attended = jnp.einsum('hqk,khd->qhd', prob_rounded, value_rows).astype(jnp.bfloat16).reshape(row_count, attn_width)
    grad_attended = jnp.dot(upstream, weights[:, 3 * attn_width:], preferred_element_type=jnp.float32).astype(jnp.bfloat16)
    grad_heads = grad_attended.reshape(row_count, head_count, HEAD_DIM).astype(jnp.float32)
    grad_prob = jnp.einsum('qhd,khd->hqk', grad_heads, value_rows)
    delta = lax.optimization_barrier(jnp.sum(probabilities * grad_prob, axis=-1, keepdims=True))
    grad_score = (probabilities * (grad_prob - delta) * scaling).astype(jnp.bfloat16).astype(jnp.float32)
    grad_query = jnp.einsum('hqk,khd->qhd', grad_score, key_rows)
    grad_key = jnp.einsum('hqk,qhd->khd', grad_score, queries)
    grad_value = jnp.einsum('hqk,qhd->khd', prob_rounded, grad_heads)
    grad_qkv = jnp.concatenate([grad_query.reshape(row_count, attn_width), grad_key.reshape(row_count, attn_width), grad_value.reshape(row_count, attn_width)], axis=1).astype(jnp.bfloat16)
    grad_normed = lax.dot_general(grad_qkv, projection, (((1,), (1,)), ((), ())), preferred_element_type=jnp.float32)
    grad_inputs = upstream.astype(jnp.float32) + norm_scale * grad_normed - values * norm_scale ** 3 * lax.optimization_barrier(jnp.mean(values * grad_normed, axis=-1, keepdims=True))
    return (grad_inputs.astype(jnp.bfloat16), normed, grad_qkv, attended)

def regroup(array):
    return array.reshape(MICRO, N_FSDP, ROWS, array.shape[-1]).transpose(1, 0, 2, 3).reshape(N_FSDP, MICRO * ROWS, array.shape[-1])

def weight_grad(normed, grad_qkv, upstream, attended):

    def accumulate(total, block):
        block_normed, block_qkv, block_up, block_att = block
        first = jnp.dot(block_normed.T, block_qkv, preferred_element_type=jnp.float32)
        second = jnp.dot(block_up.T, block_att, preferred_element_type=jnp.float32)
        partial_sum = lax.optimization_barrier(jnp.concatenate([first, second], axis=1).astype(jnp.bfloat16)).astype(jnp.float32)
        return (total + partial_sum, None)
    start = jnp.zeros((D, 4 * AW), jnp.float32)
    total, _ = lax.scan(accumulate, start, (regroup(normed), regroup(grad_qkv), regroup(upstream), regroup(attended)))
    return total

def reference(saved_inputs, attn_weights, grad_out, segments, coords, embed_in, embed_out):
    item_count = MICRO * N_FSDP
    segment_rows = segments.reshape(item_count, ROWS)
    upstream = grad_out.reshape(item_count, ROWS, D)
    layer_grads = []
    for layer in range(LAYERS - 1, -1, -1):
        inputs = saved_inputs[layer].reshape(item_count, ROWS, D)
        grad_inputs, normed, grad_qkv, attended = jax.vmap(layer_backward, in_axes=(0, 0, 0, None))(inputs, upstream, segment_rows, attn_weights[layer])
        layer_grads.append(weight_grad(normed.reshape(item_count * ROWS, D), grad_qkv.reshape(item_count * ROWS, 3 * AW), upstream.reshape(item_count * ROWS, D), attended.reshape(item_count * ROWS, AW)))
        upstream = grad_inputs
    attn_grad = jnp.stack(layer_grads[::-1])
    input_grad = upstream.reshape(MICRO, N_FSDP * ROWS, D)
    augmented = jnp.concatenate([coords, jnp.ones((1, MICRO, N_FSDP * ROWS), jnp.float32)], axis=0)
    aug_blocks = augmented.reshape(4, MICRO, N_FSDP, ROWS).transpose(2, 0, 1, 3).reshape(N_FSDP, 4, MICRO * ROWS)
    grad_blocks = regroup(input_grad.reshape(MICRO * N_FSDP * ROWS, D))
    embed_in_f = embed_in.astype(jnp.float32)

    def accumulate(totals, block):
        aug_rows, grad_rows = block
        pre = jnp.dot(embed_in_f, aug_rows, precision=lax.Precision.HIGHEST)
        hidden = gelu_value(pre).astype(jnp.bfloat16)
        term_out = jnp.dot(hidden, grad_rows, preferred_element_type=jnp.float32)
        grad_hidden = lax.dot_general(embed_out, grad_rows, (((1,), (1,)), ((), ())), preferred_element_type=jnp.float32)
        grad_pre = grad_hidden * gelu_slope(pre)
        term_in = lax.dot_general(grad_pre, aug_rows, (((1,), (1,)), ((), ())), precision=lax.Precision.HIGHEST)
        term_out = lax.optimization_barrier(term_out.astype(jnp.bfloat16)).astype(jnp.float32)
        term_in = lax.optimization_barrier(term_in.astype(jnp.bfloat16)).astype(jnp.float32)
        return ((totals[0] + term_out, totals[1] + term_in), None)
    start = (jnp.zeros((HID, D), jnp.float32), jnp.zeros((HID, 4), jnp.float32))
    totals, _ = lax.scan(accumulate, start, (aug_blocks, grad_blocks))
    return (attn_grad, input_grad, totals[0], totals[1])
```

```python
import jax
import jax.numpy as jnp
from jax import lax
from jax.sharding import PartitionSpec as P

HEAD_DIM = 64


EPS = 1e-05


def gelu_value(pre):
    return 0.5 * pre * (1.0 + jax.scipy.special.erf(pre / jnp.sqrt(2.0)))


def gelu_slope(pre):
    return 0.5 * (1.0 + jax.scipy.special.erf(pre / jnp.sqrt(2.0))) + pre * jnp.exp(
        -0.5 * pre * pre
    ) / jnp.sqrt(2.0 * jnp.pi)


def normalize(inputs):
    values = inputs.astype(jnp.float32)
    norm_scale = lax.rsqrt(jnp.mean(values * values, axis=-1, keepdims=True) + EPS)
    normed = (values * norm_scale).astype(jnp.bfloat16)
    return (norm_scale, normed)


def layer_backward(inputs, upstream, segment, weights, blocks):
    row_count = inputs.shape[0]
    block_rows = row_count // blocks
    attn_width = weights.shape[1] // 4
    head_count = attn_width // HEAD_DIM
    scaling = HEAD_DIM ** (-0.5)
    values = inputs.astype(jnp.float32)
    projection = weights[:, : 3 * attn_width]
    norm_scale, normed = normalize(inputs)
    projected = jnp.dot(normed, projection, preferred_element_type=jnp.float32).astype(jnp.bfloat16)
    shape4 = (blocks, block_rows, head_count, HEAD_DIM)
    queries = projected[:, :attn_width].reshape(shape4)
    key_rows = projected[:, attn_width : 2 * attn_width].reshape(shape4)
    value_rows = projected[:, 2 * attn_width :].reshape(shape4)
    scores = (
        jnp.einsum("bqhd,bkhd->bhqk", queries, key_rows, preferred_element_type=jnp.float32)
        * scaling
    )
    same_session = segment[:, :, None] == segment[:, None, :]
    scores = jnp.where(same_session[:, None], scores, -1e30)
    row_peak = jnp.max(scores, axis=-1, keepdims=True)
    exponent = jnp.exp(scores - row_peak)
    probabilities = exponent / jnp.sum(exponent, axis=-1, keepdims=True)
    prob_rounded = probabilities.astype(jnp.bfloat16)
    attended = (
        jnp.einsum("bhqk,bkhd->bqhd", prob_rounded, value_rows, preferred_element_type=jnp.float32)
        .astype(jnp.bfloat16)
        .reshape(row_count, attn_width)
    )
    grad_attended = jnp.dot(
        upstream, weights[:, 3 * attn_width :], preferred_element_type=jnp.float32
    ).astype(jnp.bfloat16)
    grad_heads = grad_attended.reshape(shape4)
    grad_prob = jnp.einsum(
        "bqhd,bkhd->bhqk", grad_heads, value_rows, preferred_element_type=jnp.float32
    )
    delta = jnp.sum(probabilities * grad_prob, axis=-1, keepdims=True)
    grad_score = (probabilities * (grad_prob - delta) * scaling).astype(jnp.bfloat16)
    grad_query = jnp.einsum(
        "bhqk,bkhd->bqhd", grad_score, key_rows, preferred_element_type=jnp.float32
    )
    grad_key = jnp.einsum(
        "bhqk,bqhd->bkhd", grad_score, queries, preferred_element_type=jnp.float32
    )
    grad_value = jnp.einsum(
        "bhqk,bqhd->bkhd", prob_rounded, grad_heads, preferred_element_type=jnp.float32
    )
    grad_qkv = jnp.concatenate(
        [
            grad_query.reshape(row_count, attn_width),
            grad_key.reshape(row_count, attn_width),
            grad_value.reshape(row_count, attn_width),
        ],
        axis=1,
    ).astype(jnp.bfloat16)
    grad_normed = lax.dot_general(
        grad_qkv, projection, (((1,), (1,)), ((), ())), preferred_element_type=jnp.float32
    )
    grad_inputs = (
        upstream.astype(jnp.float32)
        + norm_scale * grad_normed
        - values * norm_scale**3 * jnp.mean(values * grad_normed, axis=-1, keepdims=True)
    )
    return (grad_inputs.astype(jnp.bfloat16), normed, grad_qkv, attended)


def embed_terms(embed_in_q, embed_out_q, aug_rows, grad_rows):
    pre = jnp.dot(embed_in_q.astype(jnp.float32), aug_rows, precision=lax.Precision.HIGHEST)
    hidden = gelu_value(pre).astype(jnp.bfloat16)
    term_out = jnp.dot(hidden, grad_rows, preferred_element_type=jnp.float32)
    grad_hidden = lax.dot_general(
        embed_out_q, grad_rows, (((1,), (1,)), ((), ())), preferred_element_type=jnp.float32
    )
    grad_pre = grad_hidden * gelu_slope(pre)
    term_in = lax.dot_general(
        grad_pre, aug_rows, (((1,), (1,)), ((), ())), precision=lax.Precision.HIGHEST
    )
    return (term_out, term_in)


def broadcast_from_first(block, axis):
    count = lax.axis_size(axis)
    index = lax.axis_index(axis)
    if count == 1:
        return block
    result = jnp.where(index == 0, block, lax.ppermute(block, axis, [(0, 1)]))
    if count > 2:
        back = lax.ppermute(block, axis, [(0, count - 1)])
        result = jnp.where(index == count - 1, back, result)
    if count <= 3:
        return result
    assert count == 4
    half = block.shape[0] // 2
    low = lax.ppermute(result[:half], axis, [(1, 2)])
    high = lax.ppermute(result[half:], axis, [(3, 2)])
    return jnp.where(index == 2, jnp.concatenate([low, high], axis=0), result)


def on_device(saved_inputs, attn_weights, grad_out, segments, coords, embed_in, embed_out):
    section_count = lax.axis_size("section")
    section_index = lax.axis_index("section")
    fsdp_count = lax.axis_size("fsdp")
    micro_count = saved_inputs.shape[1]
    row_count = saved_inputs.shape[2]
    width = saved_inputs.shape[3]
    attn_width = attn_weights.shape[2] // 4
    all_rows = micro_count * row_count
    embed_rows = embed_out.shape[0]

    whole_layer = lax.all_gather(attn_weights[0], "fsdp", axis=0, tiled=True)
    embed_both = lax.all_gather(
        jnp.concatenate([embed_out, embed_in], axis=1), "fsdp", axis=0, tiled=True
    )
    embed_out_q = embed_both[:, :width]
    embed_in_q = embed_both[:, width:]
    augmented = jnp.concatenate(
        [
            coords.reshape(3, all_rows),
            jnp.ones((1, all_rows), jnp.float32),
        ],
        axis=0,
    )
    inputs = saved_inputs[0].reshape(all_rows, width)
    segment = segments[:, 0, :]
    top_grad = grad_out.reshape(all_rows, width)

    received = top_grad
    keep = None
    for step_index in range(section_count):
        active = section_count - 1 - step_index
        upstream = top_grad if step_index == 0 else received
        grad_inputs, normed, grad_qkv, attended = layer_backward(
            inputs, upstream, segment, whole_layer, micro_count
        )
        fresh = (normed, grad_qkv, upstream, attended, grad_inputs)
        if keep is None:
            keep = fresh
        else:
            valid = section_index == active
            keep = tuple(jnp.where(valid, f, k) for f, k in zip(fresh, keep))
        if step_index < section_count - 1:
            pairs = [(i, i - 1) for i in range(1, section_count)]
            received = lax.ppermute(grad_inputs, "section", pairs)
    normed_all, qkv_all, up_all, att_all, first_grad = keep
    first = lax.dot_general(
        normed_all, qkv_all, (((0,), (0,)), ((), ())), preferred_element_type=jnp.float32
    )
    second = lax.dot_general(
        up_all, att_all, (((0,), (0,)), ((), ())), preferred_element_type=jnp.float32
    )
    attn_grad = lax.psum_scatter(
        jnp.concatenate([first, second], axis=1).astype(jnp.bfloat16),
        "fsdp",
        scatter_dimension=0,
        tiled=True,
    ).astype(jnp.float32)
    input_grad = broadcast_from_first(first_grad, "section")
    term_out, term_in = embed_terms(embed_in_q, embed_out_q, augmented, input_grad)
    terms = jnp.concatenate([term_out, term_in], axis=1).astype(jnp.bfloat16)
    share = embed_rows
    pieces = lax.all_to_all(
        terms.reshape(fsdp_count, share, terms.shape[1]), "fsdp", 0, 0, tiled=False
    )
    summed = jnp.sum(pieces.astype(jnp.float32), axis=0)
    embed_out_grad = summed[:, :width]
    embed_in_grad = summed[:, width:]
    return (
        attn_grad[None],
        input_grad.reshape(micro_count, row_count, width),
        embed_out_grad,
        embed_in_grad,
    )


def solution(mesh):
    placed = (
        P("section", None, "fsdp", None),
        P("section", "fsdp", None),
        P(None, "fsdp", None),
        P(None, "fsdp", None),
        P(None, None, "fsdp"),
        P(("section", "fsdp"), None),
        P(("section", "fsdp"), None),
    )
    return jax.shard_map(
        on_device,
        mesh=mesh,
        in_specs=placed,
        out_specs=(
            P("section", "fsdp", None),
            P(None, "fsdp", None),
            P(("section", "fsdp"), None),
            P(("section", "fsdp"), None),
        ),
        check_vma=False,
    )
```

```python
import jax
import jax.numpy as jnp
from jax import lax
from jax.sharding import Mesh, NamedSharding, PartitionSpec as P

HEAD_DIM = 64


EPS = 1e-05

FSDP = ("xy", "core")


def gelu_value(pre):
    return 0.5 * pre * (1.0 + jax.scipy.special.erf(pre / jnp.sqrt(2.0)))


def gelu_slope(pre):
    return 0.5 * (1.0 + jax.scipy.special.erf(pre / jnp.sqrt(2.0))) + pre * jnp.exp(
        -0.5 * pre * pre
    ) / jnp.sqrt(2.0 * jnp.pi)


def normalize(inputs):
    values = inputs.astype(jnp.float32)
    norm_scale = lax.rsqrt(jnp.mean(values * values, axis=-1, keepdims=True) + EPS)
    normed = (values * norm_scale).astype(jnp.bfloat16)
    return (norm_scale, normed)


def swap_cores(value):
    return lax.ppermute(value, "core", [(0, 1), (1, 0)])


def pick(value, index, axis):
    return lax.dynamic_index_in_dim(value, index, axis, keepdims=False)


def attention_forward(normed, weights_qkv, segment, blocks):
    row_count = normed.shape[0]
    width = weights_qkv.shape[2]
    heads = width // HEAD_DIM
    scaling = HEAD_DIM ** (-0.5)
    projected = jnp.dot(
        normed, weights_qkv.reshape(weights_qkv.shape[0], 3 * width),
        preferred_element_type=jnp.float32,
    ).astype(jnp.bfloat16)
    shape4 = (blocks, row_count // blocks, heads, HEAD_DIM)
    queries = projected[:, :width].reshape(shape4)
    key_rows = projected[:, width : 2 * width].reshape(shape4)
    value_rows = projected[:, 2 * width :].reshape(shape4)
    scores = (
        jnp.einsum("bqhd,bkhd->bhqk", queries, key_rows, preferred_element_type=jnp.float32)
        * scaling
    )
    same_session = segment[:, :, None] == segment[:, None, :]
    scores = jnp.where(same_session[:, None], scores, -1e30)
    row_peak = jnp.max(scores, axis=-1, keepdims=True)
    exponent = jnp.exp(scores - row_peak)
    probabilities = exponent / jnp.sum(exponent, axis=-1, keepdims=True)
    prob_rounded = probabilities.astype(jnp.bfloat16)
    attended = (
        jnp.einsum("bhqk,bkhd->bqhd", prob_rounded, value_rows, preferred_element_type=jnp.float32)
        .astype(jnp.bfloat16)
        .reshape(row_count, width)
    )
    return queries, key_rows, value_rows, probabilities, prob_rounded, attended


def attention_backward(forward, upstream, weights_qkv, weights_out):
    queries, key_rows, value_rows, probabilities, prob_rounded, _ = forward
    row_count = upstream.shape[0]
    width = weights_out.shape[1]
    scaling = HEAD_DIM ** (-0.5)
    grad_attended = jnp.dot(
        upstream, weights_out, preferred_element_type=jnp.float32
    ).astype(jnp.bfloat16)
    grad_heads = grad_attended.reshape(queries.shape)
    grad_prob = jnp.einsum(
        "bqhd,bkhd->bhqk", grad_heads, value_rows, preferred_element_type=jnp.float32
    )
    delta = jnp.sum(probabilities * grad_prob, axis=-1, keepdims=True)
    grad_score = (probabilities * (grad_prob - delta) * scaling).astype(jnp.bfloat16)
    grad_query = jnp.einsum(
        "bhqk,bkhd->bqhd", grad_score, key_rows, preferred_element_type=jnp.float32
    )
    grad_key = jnp.einsum(
        "bhqk,bqhd->bkhd", grad_score, queries, preferred_element_type=jnp.float32
    )
    grad_value = jnp.einsum(
        "bhqk,bqhd->bkhd", prob_rounded, grad_heads, preferred_element_type=jnp.float32
    )
    grad_qkv = jnp.concatenate(
        [
            grad_query.reshape(row_count, width),
            grad_key.reshape(row_count, width),
            grad_value.reshape(row_count, width),
        ],
        axis=1,
    ).astype(jnp.bfloat16)
    grad_normed = lax.dot_general(
        grad_qkv,
        weights_qkv.reshape(weights_qkv.shape[0], 3 * width),
        (((1,), (1,)), ((), ())),
        preferred_element_type=jnp.float32,
    )
    return grad_qkv, grad_normed


def embed_terms(embed_in_q, embed_out_q, aug_rows, grad_rows):
    pre = jnp.dot(embed_in_q.astype(jnp.float32), aug_rows, precision=lax.Precision.HIGHEST)
    hidden = gelu_value(pre).astype(jnp.bfloat16)
    term_out = jnp.dot(hidden, grad_rows, preferred_element_type=jnp.float32)
    grad_hidden = lax.dot_general(
        embed_out_q, grad_rows, (((1,), (1,)), ((), ())), preferred_element_type=jnp.float32
    )
    grad_pre = grad_hidden * gelu_slope(pre)
    term_in = lax.dot_general(
        grad_pre, aug_rows, (((1,), (1,)), ((), ())), precision=lax.Precision.HIGHEST
    )
    return (term_out, term_in)


def broadcast_from_first(block, axis):
    count = lax.axis_size(axis)
    index = lax.axis_index(axis)
    if count == 1:
        return block
    result = jnp.where(index == 0, block, lax.ppermute(block, axis, [(0, 1)]))
    if count > 2:
        back = lax.ppermute(block, axis, [(0, count - 1)])
        result = jnp.where(index == count - 1, back, result)
    if count <= 3:
        return result
    assert count == 4
    half = block.shape[0] // 2
    low = lax.ppermute(result[:half], axis, [(1, 2)])
    high = lax.ppermute(result[half:], axis, [(3, 2)])
    return jnp.where(index == 2, jnp.concatenate([low, high], axis=0), result)


def on_device(saved_inputs, attn_weights, grad_out, segments, coords, embed_in, embed_out):
    section_count = lax.axis_size("section")
    section_index = lax.axis_index("section")
    chip_count = lax.axis_size("xy")
    core = lax.axis_index("core")
    other = 1 - core
    micro_count = saved_inputs.shape[1]
    row_count = saved_inputs.shape[2]
    width = saved_inputs.shape[3]
    local_rows = attn_weights.shape[1]
    attn_width = attn_weights.shape[2] // 4
    half_width = attn_width // 2
    own_rows = micro_count * row_count
    embed_rows = embed_out.shape[0]

    mine = attn_weights[0].reshape(local_rows, 4, 2, half_width)
    given = swap_cores(pick(mine, other, 2))
    kept = pick(mine, core, 2)
    chip_rows = jnp.where(
        core == 0,
        jnp.concatenate([kept, given], axis=0),
        jnp.concatenate([given, kept], axis=0),
    )
    layer = lax.all_gather(chip_rows, "xy", axis=0, tiled=True)
    weights_qkv = layer[:, :3, :]
    weights_out = layer[:, 3, :]

    embed_both = lax.all_gather(
        jnp.concatenate([embed_out, embed_in], axis=1), FSDP, axis=0, tiled=True
    )

    inputs_own = saved_inputs[0].reshape(own_rows, width)
    inputs_all = jnp.concatenate([inputs_own, swap_cores(inputs_own)], axis=0)
    segment_own = segments[:, 0, :]
    segment_all = jnp.concatenate([segment_own, swap_cores(segment_own)], axis=0)
    norm_scale_all, normed_all = normalize(inputs_all)
    norm_scale = norm_scale_all[:own_rows]
    values = inputs_own.astype(jnp.float32)
    forward = attention_forward(normed_all, weights_qkv, segment_all, 2 * micro_count)
    attended_all = forward[-1]

    top_grad = grad_out.reshape(own_rows, width)
    received = top_grad
    keep = None
    for step_index in range(section_count):
        active = section_count - 1 - step_index
        upstream = top_grad if step_index == 0 else received
        upstream_all = jnp.concatenate([upstream, swap_cores(upstream)], axis=0)
        grad_qkv, grad_normed = attention_backward(
            forward, upstream_all, weights_qkv, weights_out
        )
        grad_normed = grad_normed[:own_rows] + swap_cores(grad_normed[own_rows:])
        grad_inputs = (
            upstream.astype(jnp.float32)
            + norm_scale * grad_normed
            - values * norm_scale**3 * jnp.mean(values * grad_normed, axis=-1, keepdims=True)
        ).astype(jnp.bfloat16)
        fresh = (grad_qkv, upstream_all, grad_inputs)
        if keep is None:
            keep = fresh
        else:
            valid = section_index == active
            keep = tuple(jnp.where(valid, f, k) for f, k in zip(fresh, keep))
        if step_index < section_count - 1:
            pairs = [(i, i - 1) for i in range(1, section_count)]
            received = lax.ppermute(grad_inputs, "section", pairs)
    qkv_all, up_all, first_grad = keep
    first = lax.dot_general(
        normed_all, qkv_all, (((0,), (0,)), ((), ())), preferred_element_type=jnp.float32
    )
    second = lax.dot_general(
        up_all, attended_all, (((0,), (0,)), ((), ())), preferred_element_type=jnp.float32
    )
    grad_half = jnp.concatenate(
        [first.reshape(width, 3, half_width), second.reshape(width, 1, half_width)], axis=1
    ).astype(jnp.bfloat16)
    chip_grad = lax.psum_scatter(grad_half, "xy", scatter_dimension=0, tiled=True)
    chip_grad = chip_grad.reshape(2, local_rows, 4, half_width)
    mine_grad = pick(chip_grad, core, 0)
    theirs_grad = swap_cores(pick(chip_grad, other, 0))
    attn_grad = jnp.where(
        core == 0,
        jnp.stack([mine_grad, theirs_grad], axis=2),
        jnp.stack([theirs_grad, mine_grad], axis=2),
    ).reshape(local_rows, 4 * attn_width).astype(jnp.float32)

    input_grad = broadcast_from_first(first_grad, "section")
    grad_all = jnp.concatenate([input_grad, swap_cores(input_grad)], axis=0)
    coords_own = coords.reshape(3, own_rows)
    coords_all = jnp.concatenate([coords_own, swap_cores(coords_own)], axis=1)
    augmented = jnp.concatenate(
        [coords_all, jnp.ones((1, 2 * own_rows), jnp.float32)], axis=0
    )
    embed_half = pick(
        embed_both.reshape(chip_count, 2, embed_rows, width + embed_in.shape[1]), core, 1
    ).reshape(chip_count * embed_rows, width + embed_in.shape[1])
    term_out, term_in = embed_terms(
        embed_half[:, width:], embed_half[:, :width], augmented, grad_all
    )
    terms = jnp.concatenate([term_out, term_in], axis=1).astype(jnp.bfloat16)
    pieces = lax.all_to_all(
        terms.reshape(chip_count, embed_rows, terms.shape[1]), "xy", 0, 0, tiled=False
    )
    summed = jnp.sum(pieces.astype(jnp.float32), axis=0)
    return (
        attn_grad[None],
        input_grad.reshape(micro_count, row_count, width),
        summed[:, :width],
        summed[:, width:],
    )


def solution(mesh):
    sections, fsdp = mesh.devices.shape
    inner = Mesh(mesh.devices.reshape(sections, fsdp // 2, 2), ("section", "xy", "core"))
    placed = (
        P("section", None, FSDP, None),
        P("section", FSDP, None),
        P(None, FSDP, None),
        P(None, FSDP, None),
        P(None, None, FSDP),
        P(("section",) + FSDP, None),
        P(("section",) + FSDP, None),
    )
    outer_specs = (
        P("section", "fsdp", None),
        P(None, "fsdp", None),
        P(("section", "fsdp"), None),
        P(("section", "fsdp"), None),
    )
    mapped = jax.shard_map(
        on_device,
        mesh=inner,
        in_specs=placed,
        out_specs=(
            P("section", FSDP, None),
            P(None, FSDP, None),
            P(("section",) + FSDP, None),
            P(("section",) + FSDP, None),
        ),
        check_vma=False,
    )

    def run(*args):
        outs = mapped(*args)
        return tuple(
            lax.with_sharding_constraint(o, NamedSharding(mesh, s))
            for o, s in zip(outs, outer_specs)
        )

    return run
```

```python
import jax
import jax.numpy as jnp
from jax import lax
from jax.sharding import Mesh, NamedSharding, PartitionSpec as P

HEAD_DIM = 64


EPS = 1e-05

FSDP = ("xy", "core")


def gelu_value(pre):
    return 0.5 * pre * (1.0 + jax.scipy.special.erf(pre / jnp.sqrt(2.0)))


def gelu_slope(pre):
    return 0.5 * (1.0 + jax.scipy.special.erf(pre / jnp.sqrt(2.0))) + pre * jnp.exp(
        -0.5 * pre * pre
    ) / jnp.sqrt(2.0 * jnp.pi)


def normalize(inputs):
    values = inputs.astype(jnp.float32)
    norm_scale = lax.rsqrt(jnp.mean(values * values, axis=-1, keepdims=True) + EPS)
    normed = (values * norm_scale).astype(jnp.bfloat16)
    return (norm_scale, normed)


def swap_cores(value):
    return lax.ppermute(value, "core", [(0, 1), (1, 0)])


def pick(value, index, axis):
    return lax.dynamic_index_in_dim(value, index, axis, keepdims=False)


def attention_forward(normed, weights_qkv, segment, blocks):
    row_count = normed.shape[0]
    width = weights_qkv.shape[1] // 3
    heads = width // HEAD_DIM
    scaling = HEAD_DIM ** (-0.5)
    projected = jnp.dot(
        normed, weights_qkv, preferred_element_type=jnp.float32
    ).astype(jnp.bfloat16)
    shape4 = (blocks, row_count // blocks, heads, HEAD_DIM)
    queries = projected[:, :width].reshape(shape4)
    key_rows = projected[:, width : 2 * width].reshape(shape4)
    value_rows = projected[:, 2 * width :].reshape(shape4)
    scores = (
        jnp.einsum("bqhd,bkhd->bhqk", queries, key_rows, preferred_element_type=jnp.float32)
        * scaling
    )
    same_session = segment[:, :, None] == segment[:, None, :]
    scores = jnp.where(same_session[:, None], scores, -1e30)
    row_peak = jnp.max(scores, axis=-1, keepdims=True)
    exponent = jnp.exp(scores - row_peak)
    probabilities = exponent / jnp.sum(exponent, axis=-1, keepdims=True)
    prob_rounded = probabilities.astype(jnp.bfloat16)
    attended = (
        jnp.einsum("bhqk,bkhd->bqhd", prob_rounded, value_rows, preferred_element_type=jnp.float32)
        .astype(jnp.bfloat16)
        .reshape(row_count, width)
    )
    return queries, key_rows, value_rows, probabilities, prob_rounded, attended


def attention_backward(forward, upstream, weights_qkv, weights_out):
    queries, key_rows, value_rows, probabilities, prob_rounded, _ = forward
    row_count = upstream.shape[0]
    width = weights_out.shape[1]
    scaling = HEAD_DIM ** (-0.5)
    grad_attended = jnp.dot(
        upstream, weights_out, preferred_element_type=jnp.float32
    ).astype(jnp.bfloat16)
    grad_heads = grad_attended.reshape(queries.shape)
    grad_prob = jnp.einsum(
        "bqhd,bkhd->bhqk", grad_heads, value_rows, preferred_element_type=jnp.float32
    )
    delta = jnp.sum(probabilities * grad_prob, axis=-1, keepdims=True)
    grad_score = (probabilities * (grad_prob - delta) * scaling).astype(jnp.bfloat16)
    grad_query = jnp.einsum(
        "bhqk,bkhd->bqhd", grad_score, key_rows, preferred_element_type=jnp.float32
    )
    grad_key = jnp.einsum(
        "bhqk,bqhd->bkhd", grad_score, queries, preferred_element_type=jnp.float32
    )
    grad_value = jnp.einsum(
        "bhqk,bqhd->bkhd", prob_rounded, grad_heads, preferred_element_type=jnp.float32
    )
    grad_qkv = jnp.concatenate(
        [
            grad_query.reshape(row_count, width),
            grad_key.reshape(row_count, width),
            grad_value.reshape(row_count, width),
        ],
        axis=1,
    ).astype(jnp.bfloat16)
    grad_normed = lax.dot_general(
        grad_qkv,
        weights_qkv,
        (((1,), (1,)), ((), ())),
        preferred_element_type=jnp.float32,
    )
    return grad_qkv, grad_normed


def embed_terms(embed_in_q, embed_out_q, aug_rows, grad_rows):
    pre = jnp.dot(embed_in_q.astype(jnp.float32), aug_rows, precision=lax.Precision.HIGHEST)
    hidden = gelu_value(pre).astype(jnp.bfloat16)
    term_out = jnp.dot(hidden, grad_rows, preferred_element_type=jnp.float32)
    grad_hidden = lax.dot_general(
        embed_out_q, grad_rows, (((1,), (1,)), ((), ())), preferred_element_type=jnp.float32
    )
    grad_pre = grad_hidden * gelu_slope(pre)
    term_in = lax.dot_general(
        grad_pre, aug_rows, (((1,), (1,)), ((), ())), precision=lax.Precision.HIGHEST
    )
    return (term_out, term_in)


def broadcast_from_first(block, axis):
    count = lax.axis_size(axis)
    index = lax.axis_index(axis)
    if count == 1:
        return block
    result = jnp.where(index == 0, block, lax.ppermute(block, axis, [(0, 1)]))
    if count > 2:
        back = lax.ppermute(block, axis, [(0, count - 1)])
        result = jnp.where(index == count - 1, back, result)
    if count <= 3:
        return result
    assert count == 4
    half = block.shape[0] // 2
    low = lax.ppermute(result[:half], axis, [(1, 2)])
    high = lax.ppermute(result[half:], axis, [(3, 2)])
    return jnp.where(index == 2, jnp.concatenate([low, high], axis=0), result)


def on_device(saved_inputs, attn_weights, grad_out, segments, coords, embed_in, embed_out):
    section_count = lax.axis_size("section")
    section_index = lax.axis_index("section")
    chip_count = lax.axis_size("xy")
    core = lax.axis_index("core")
    other = 1 - core
    micro_count = saved_inputs.shape[1]
    row_count = saved_inputs.shape[2]
    width = saved_inputs.shape[3]
    local_rows = attn_weights.shape[1]
    attn_width = attn_weights.shape[2] // 4
    half_width = attn_width // 2
    own_rows = micro_count * row_count
    embed_rows = embed_out.shape[0]

    mine = attn_weights[0].reshape(local_rows, 4, 2, half_width)
    given = swap_cores(pick(mine, other, 2))
    kept = pick(mine, core, 2)
    chip_rows = jnp.where(
        core == 0,
        jnp.concatenate([kept, given], axis=0),
        jnp.concatenate([given, kept], axis=0),
    ).reshape(2 * local_rows, 4 * half_width)
    layer = lax.all_gather(chip_rows, "xy", axis=0, tiled=True)
    weights_qkv = layer[:, : 3 * half_width]
    weights_out = layer[:, 3 * half_width :]

    embed_both = lax.all_gather(
        jnp.concatenate([embed_out, embed_in], axis=1), FSDP, axis=0, tiled=True
    )

    inputs_own = saved_inputs[0].reshape(own_rows, width)
    inputs_all = jnp.concatenate([inputs_own, swap_cores(inputs_own)], axis=0)
    segment_own = segments[:, 0, :]
    segment_all = jnp.concatenate([segment_own, swap_cores(segment_own)], axis=0)
    norm_scale_all, normed_all = normalize(inputs_all)
    norm_scale = norm_scale_all[:own_rows]
    values = inputs_own.astype(jnp.float32)
    forward = attention_forward(normed_all, weights_qkv, segment_all, 2 * micro_count)
    attended_all = forward[-1]

    top_grad = grad_out.reshape(own_rows, width)
    received = top_grad
    keep = None
    for step_index in range(section_count):
        active = section_count - 1 - step_index
        upstream = top_grad if step_index == 0 else received
        upstream_all = jnp.concatenate([upstream, swap_cores(upstream)], axis=0)
        grad_qkv, grad_normed = attention_backward(
            forward, upstream_all, weights_qkv, weights_out
        )
        grad_normed = grad_normed[:own_rows] + swap_cores(grad_normed[own_rows:])
        grad_inputs = (
            upstream.astype(jnp.float32)
            + norm_scale * grad_normed
            - values * norm_scale**3 * jnp.mean(values * grad_normed, axis=-1, keepdims=True)
        ).astype(jnp.bfloat16)
        fresh = (grad_qkv, upstream_all, grad_inputs)
        if keep is None:
            keep = fresh
        else:
            valid = section_index == active
            keep = tuple(jnp.where(valid, f, k) for f, k in zip(fresh, keep))
        if step_index < section_count - 1:
            pairs = [(i, i - 1) for i in range(1, section_count)]
            received = lax.ppermute(grad_inputs, "section", pairs)
    qkv_all, up_all, first_grad = keep
    first = lax.dot_general(
        normed_all, qkv_all, (((0,), (0,)), ((), ())), preferred_element_type=jnp.float32
    )
    second = lax.dot_general(
        up_all, attended_all, (((0,), (0,)), ((), ())), preferred_element_type=jnp.float32
    )
    grad_half = jnp.concatenate([first, second], axis=1).astype(jnp.bfloat16)
    chip_grad = lax.psum_scatter(grad_half, "xy", scatter_dimension=0, tiled=True)
    chip_grad = chip_grad.reshape(2, local_rows, 4, half_width)
    mine_grad = pick(chip_grad, core, 0)
    theirs_grad = swap_cores(pick(chip_grad, other, 0))
    attn_grad = jnp.where(
        core == 0,
        jnp.stack([mine_grad, theirs_grad], axis=2),
        jnp.stack([theirs_grad, mine_grad], axis=2),
    ).reshape(local_rows, 4 * attn_width).astype(jnp.float32)

    input_grad = broadcast_from_first(first_grad, "section")
    grad_all = jnp.concatenate([input_grad, swap_cores(input_grad)], axis=0)
    coords_own = coords.reshape(3, own_rows)
    coords_all = jnp.concatenate([coords_own, swap_cores(coords_own)], axis=1)
    augmented = jnp.concatenate(
        [coords_all, jnp.ones((1, 2 * own_rows), jnp.float32)], axis=0
    )
    embed_half = pick(
        embed_both.reshape(chip_count, 2, embed_rows, width + embed_in.shape[1]), core, 1
    ).reshape(chip_count * embed_rows, width + embed_in.shape[1])
    term_out, term_in = embed_terms(
        embed_half[:, width:], embed_half[:, :width], augmented, grad_all
    )
    terms = jnp.concatenate([term_out, term_in], axis=1).astype(jnp.bfloat16)
    pieces = lax.all_to_all(
        terms.reshape(chip_count, embed_rows, terms.shape[1]), "xy", 0, 0, tiled=False
    )
    summed = jnp.sum(pieces.astype(jnp.float32), axis=0)
    return (
        attn_grad[None],
        input_grad.reshape(micro_count, row_count, width),
        summed[:, :width],
        summed[:, width:],
    )


def solution(mesh):
    sections, fsdp = mesh.devices.shape
    inner = Mesh(mesh.devices.reshape(sections, fsdp // 2, 2), ("section", "xy", "core"))
    placed = (
        P("section", None, FSDP, None),
        P("section", FSDP, None),
        P(None, FSDP, None),
        P(None, FSDP, None),
        P(None, None, FSDP),
        P(("section",) + FSDP, None),
        P(("section",) + FSDP, None),
    )
    outer_specs = (
        P("section", "fsdp", None),
        P(None, "fsdp", None),
        P(("section", "fsdp"), None),
        P(("section", "fsdp"), None),
    )
    mapped = jax.shard_map(
        on_device,
        mesh=inner,
        in_specs=placed,
        out_specs=(
            P("section", FSDP, None),
            P(None, FSDP, None),
            P(("section",) + FSDP, None),
            P(("section",) + FSDP, None),
        ),
        check_vma=False,
    )

    def run(*args):
        outs = mapped(*args)
        return tuple(
            lax.with_sharding_constraint(o, NamedSharding(mesh, s))
            for o, s in zip(outs, outer_specs)
        )

    return run
```

```python
import jax
import jax.numpy as jnp
from jax import lax
from jax.sharding import Mesh, NamedSharding, PartitionSpec as P

HEAD_DIM = 64


EPS = 1e-05

FSDP = ("xy", "core")


def gelu_value(pre):
    return 0.5 * pre * (1.0 + jax.scipy.special.erf(pre / jnp.sqrt(2.0)))


def gelu_slope(pre):
    return 0.5 * (1.0 + jax.scipy.special.erf(pre / jnp.sqrt(2.0))) + pre * jnp.exp(
        -0.5 * pre * pre
    ) / jnp.sqrt(2.0 * jnp.pi)


def normalize(inputs):
    values = inputs.astype(jnp.float32)
    norm_scale = lax.rsqrt(jnp.mean(values * values, axis=-1, keepdims=True) + EPS)
    normed = (values * norm_scale).astype(jnp.bfloat16)
    return (norm_scale, normed)


def swap_cores(value):
    return lax.ppermute(value, "core", [(0, 1), (1, 0)])


def pick(value, index, axis):
    return lax.dynamic_index_in_dim(value, index, axis, keepdims=False)


def attention_forward(normed, weights_qkv, segment, blocks):
    row_count = normed.shape[0]
    width = weights_qkv.shape[1] // 3
    heads = width // HEAD_DIM
    scaling = HEAD_DIM ** (-0.5)
    projected = jnp.dot(
        normed, weights_qkv, preferred_element_type=jnp.float32
    ).astype(jnp.bfloat16)
    shape4 = (blocks, row_count // blocks, heads, HEAD_DIM)
    queries = projected[:, :width].reshape(shape4)
    key_rows = projected[:, width : 2 * width].reshape(shape4)
    value_rows = projected[:, 2 * width :].reshape(shape4)
    scores = (
        jnp.einsum("bqhd,bkhd->bhqk", queries, key_rows, preferred_element_type=jnp.float32)
        * scaling
    )
    same_session = segment[:, :, None] == segment[:, None, :]
    scores = jnp.where(same_session[:, None], scores, -1e30)
    row_peak = jnp.max(scores, axis=-1, keepdims=True)
    exponent = jnp.exp(scores - row_peak)
    probabilities = exponent / jnp.sum(exponent, axis=-1, keepdims=True)
    prob_rounded = probabilities.astype(jnp.bfloat16)
    attended = (
        jnp.einsum("bhqk,bkhd->bqhd", prob_rounded, value_rows, preferred_element_type=jnp.float32)
        .astype(jnp.bfloat16)
        .reshape(row_count, width)
    )
    return queries, key_rows, value_rows, probabilities, prob_rounded, attended


def attention_backward(forward, upstream, weights_qkv, weights_out):
    queries, key_rows, value_rows, probabilities, prob_rounded, _ = forward
    row_count = upstream.shape[0]
    width = weights_out.shape[1]
    scaling = HEAD_DIM ** (-0.5)
    grad_attended = jnp.dot(
        upstream, weights_out, preferred_element_type=jnp.float32
    ).astype(jnp.bfloat16)
    grad_heads = grad_attended.reshape(queries.shape)
    grad_prob = jnp.einsum(
        "bqhd,bkhd->bhqk", grad_heads, value_rows, preferred_element_type=jnp.float32
    )
    delta = jnp.sum(probabilities * grad_prob, axis=-1, keepdims=True)
    grad_score = (probabilities * (grad_prob - delta) * scaling).astype(jnp.bfloat16)
    grad_query = jnp.einsum(
        "bhqk,bkhd->bqhd", grad_score, key_rows, preferred_element_type=jnp.float32
    )
    grad_key = jnp.einsum(
        "bhqk,bqhd->bkhd", grad_score, queries, preferred_element_type=jnp.float32
    )
    grad_value = jnp.einsum(
        "bhqk,bqhd->bkhd", prob_rounded, grad_heads, preferred_element_type=jnp.float32
    )
    grad_qkv = jnp.concatenate(
        [
            grad_query.reshape(row_count, width),
            grad_key.reshape(row_count, width),
            grad_value.reshape(row_count, width),
        ],
        axis=1,
    ).astype(jnp.bfloat16)
    grad_normed = lax.dot_general(
        grad_qkv,
        weights_qkv,
        (((1,), (1,)), ((), ())),
        preferred_element_type=jnp.float32,
    )
    return grad_qkv, grad_normed


def embed_terms(embed_in_q, embed_out_q, aug_rows, grad_rows):
    pre = jnp.dot(embed_in_q.astype(jnp.float32), aug_rows, precision=lax.Precision.HIGHEST)
    hidden = gelu_value(pre).astype(jnp.bfloat16)
    term_out = jnp.dot(hidden, grad_rows, preferred_element_type=jnp.float32)
    grad_hidden = lax.dot_general(
        embed_out_q, grad_rows, (((1,), (1,)), ((), ())), preferred_element_type=jnp.float32
    )
    grad_pre = grad_hidden * gelu_slope(pre)
    term_in = lax.dot_general(
        grad_pre, aug_rows, (((1,), (1,)), ((), ())), precision=lax.Precision.HIGHEST
    )
    return (term_out, term_in)


def broadcast_from_first(block, axis):
    count = lax.axis_size(axis)
    index = lax.axis_index(axis)
    if count == 1:
        return block
    result = jnp.where(index == 0, block, lax.ppermute(block, axis, [(0, 1)]))
    if count > 2:
        back = lax.ppermute(block, axis, [(0, count - 1)])
        result = jnp.where(index == count - 1, back, result)
    if count <= 3:
        return result
    assert count == 4
    half = block.shape[0] // 2
    low = lax.ppermute(result[:half], axis, [(1, 2)])
    high = lax.ppermute(result[half:], axis, [(3, 2)])
    return jnp.where(index == 2, jnp.concatenate([low, high], axis=0), result)


def on_device(saved_inputs, attn_weights, grad_out, segments, coords, embed_in, embed_out):
    section_count = lax.axis_size("section")
    section_index = lax.axis_index("section")
    chip_count = lax.axis_size("xy")
    core = lax.axis_index("core")
    other = 1 - core
    micro_count = saved_inputs.shape[1]
    row_count = saved_inputs.shape[2]
    width = saved_inputs.shape[3]
    local_rows = attn_weights.shape[1]
    attn_width = attn_weights.shape[2] // 4
    half_width = attn_width // 2
    own_rows = micro_count * row_count
    embed_rows = embed_out.shape[0]

    mine = attn_weights[0].reshape(local_rows, 4, 2, half_width)
    given = swap_cores(pick(mine, other, 2))
    kept = pick(mine, core, 2)
    chip_rows = jnp.where(
        core == 0,
        jnp.concatenate([kept, given], axis=0),
        jnp.concatenate([given, kept], axis=0),
    ).reshape(2 * local_rows, 4 * half_width)
    layer = lax.all_gather(chip_rows, "xy", axis=0, tiled=True)
    weights_qkv = layer[:, : 3 * half_width]
    weights_out = layer[:, 3 * half_width :]

    embed_both = lax.all_gather(
        jnp.concatenate([embed_out, embed_in], axis=1), FSDP, axis=0, tiled=True
    )

    halves = 2
    half_rows = own_rows // halves
    inputs_own = saved_inputs[0].reshape(own_rows, width)
    inputs_other = swap_cores(inputs_own)
    segment_own = segments[:, 0, :]
    segment_other = swap_cores(segment_own)
    half_micro = micro_count // halves
    parts = []
    for h in range(halves):
        rows = slice(h * half_rows, (h + 1) * half_rows)
        micros = slice(h * half_micro, (h + 1) * half_micro)
        inputs_h = jnp.concatenate([inputs_own[rows], inputs_other[rows]], axis=0)
        segment_h = jnp.concatenate([segment_own[micros], segment_other[micros]], axis=0)
        norm_scale_h, normed_h = normalize(inputs_h)
        forward_h = attention_forward(normed_h, weights_qkv, segment_h, 2 * half_micro)
        parts.append(
            dict(
                values=inputs_own[rows].astype(jnp.float32),
                norm_scale=norm_scale_h[:half_rows],
                normed_t=normed_h.T,
                forward=forward_h,
            )
        )

    top_grad = grad_out.reshape(own_rows, width)
    received = [top_grad[h * half_rows : (h + 1) * half_rows] for h in range(halves)]
    keep = None
    for step_index in range(section_count):
        active = section_count - 1 - step_index
        fresh = []
        sent = []
        for h in range(halves):
            part = parts[h]
            upstream = received[h]
            if h > 0:
                previous, upstream = lax.optimization_barrier((fresh[-1], upstream))
                fresh[-1] = previous
            upstream_all = jnp.concatenate([upstream, swap_cores(upstream)], axis=0)
            grad_qkv, grad_normed = attention_backward(
                part["forward"], upstream_all, weights_qkv, weights_out
            )
            grad_normed = grad_normed[:half_rows] + swap_cores(grad_normed[half_rows:])
            values = part["values"]
            norm_scale = part["norm_scale"]
            grad_inputs = (
                upstream.astype(jnp.float32)
                + norm_scale * grad_normed
                - values
                * norm_scale**3
                * jnp.mean(values * grad_normed, axis=-1, keepdims=True)
            ).astype(jnp.bfloat16)
            fresh.extend([grad_qkv, upstream_all, grad_inputs])
            if step_index < section_count - 1:
                pairs = [(i, i - 1) for i in range(1, section_count)]
                sent.append(lax.ppermute(grad_inputs, "section", pairs))
        if keep is None:
            keep = fresh
        else:
            valid = section_index == active
            keep = [jnp.where(valid, f, k) for f, k in zip(fresh, keep)]
        received = sent
    first = None
    second = None
    grads_own = []
    for h in range(halves):
        qkv_h, up_h, grad_h = keep[3 * h : 3 * h + 3]
        grads_own.append(grad_h)
        f = jnp.dot(parts[h]["normed_t"], qkv_h, preferred_element_type=jnp.float32)
        g = jnp.dot(up_h.T, parts[h]["forward"][-1], preferred_element_type=jnp.float32)
        first = f if first is None else first + f
        second = g if second is None else second + g
    first_grad = jnp.concatenate(grads_own, axis=0)
    grad_half = jnp.concatenate([first, second], axis=1).astype(jnp.bfloat16)
    chip_grad = lax.psum_scatter(grad_half, "xy", scatter_dimension=0, tiled=True)
    chip_grad = chip_grad.reshape(2, local_rows, 4, half_width)
    mine_grad = pick(chip_grad, core, 0)
    theirs_grad = swap_cores(pick(chip_grad, other, 0))
    attn_grad = jnp.where(
        core == 0,
        jnp.stack([mine_grad, theirs_grad], axis=2),
        jnp.stack([theirs_grad, mine_grad], axis=2),
    ).reshape(local_rows, 4 * attn_width).astype(jnp.float32)

    input_grad = broadcast_from_first(first_grad, "section")
    grad_all = jnp.concatenate([input_grad, swap_cores(input_grad)], axis=0)
    coords_own = coords.reshape(3, own_rows)
    coords_all = jnp.concatenate([coords_own, swap_cores(coords_own)], axis=1)
    augmented = jnp.concatenate(
        [coords_all, jnp.ones((1, 2 * own_rows), jnp.float32)], axis=0
    )
    embed_half = pick(
        embed_both.reshape(chip_count, 2, embed_rows, width + embed_in.shape[1]), core, 1
    ).reshape(chip_count * embed_rows, width + embed_in.shape[1])
    term_out, term_in = embed_terms(
        embed_half[:, width:], embed_half[:, :width], augmented, grad_all
    )
    terms = jnp.concatenate([term_out, term_in], axis=1).astype(jnp.bfloat16)
    pieces = lax.all_to_all(
        terms.reshape(chip_count, embed_rows, terms.shape[1]), "xy", 0, 0, tiled=False
    )
    summed = jnp.sum(pieces.astype(jnp.float32), axis=0)
    return (
        attn_grad[None],
        input_grad.reshape(micro_count, row_count, width),
        summed[:, :width],
        summed[:, width:],
    )


def solution(mesh):
    sections, fsdp = mesh.devices.shape
    inner = Mesh(mesh.devices.reshape(sections, fsdp // 2, 2), ("section", "xy", "core"))
    placed = (
        P("section", None, FSDP, None),
        P("section", FSDP, None),
        P(None, FSDP, None),
        P(None, FSDP, None),
        P(None, None, FSDP),
        P(("section",) + FSDP, None),
        P(("section",) + FSDP, None),
    )
    outer_specs = (
        P("section", "fsdp", None),
        P(None, "fsdp", None),
        P(("section", "fsdp"), None),
        P(("section", "fsdp"), None),
    )
    mapped = jax.shard_map(
        on_device,
        mesh=inner,
        in_specs=placed,
        out_specs=(
            P("section", FSDP, None),
            P(None, FSDP, None),
            P(("section",) + FSDP, None),
            P(("section",) + FSDP, None),
        ),
        check_vma=False,
    )

    def run(*args):
        outs = mapped(*args)
        return tuple(
            lax.with_sharding_constraint(o, NamedSharding(mesh, s))
            for o, s in zip(outs, outer_specs)
        )

    return run
```

```python
import jax
import jax.numpy as jnp
from jax import lax
from jax.sharding import Mesh, NamedSharding, PartitionSpec as P

HEAD_DIM = 64


EPS = 1e-05

FSDP = ("xy", "core")


def gelu_value(pre):
    return 0.5 * pre * (1.0 + jax.scipy.special.erf(pre / jnp.sqrt(2.0)))


def gelu_slope(pre):
    return 0.5 * (1.0 + jax.scipy.special.erf(pre / jnp.sqrt(2.0))) + pre * jnp.exp(
        -0.5 * pre * pre
    ) / jnp.sqrt(2.0 * jnp.pi)


def normalize(inputs):
    values = inputs.astype(jnp.float32)
    norm_scale = lax.rsqrt(jnp.mean(values * values, axis=-1, keepdims=True) + EPS)
    normed = (values * norm_scale).astype(jnp.bfloat16)
    return (norm_scale, normed)


def swap_cores(value):
    return lax.ppermute(value, "core", [(0, 1), (1, 0)])


def pick(value, index, axis):
    return lax.dynamic_index_in_dim(value, index, axis, keepdims=False)


def attention_forward(normed, weights_qkv, segment, blocks):
    row_count = normed.shape[0]
    width = weights_qkv.shape[1] // 3
    heads = width // HEAD_DIM
    scaling = HEAD_DIM ** (-0.5)
    projected = jnp.dot(
        normed, weights_qkv, preferred_element_type=jnp.float32
    ).astype(jnp.bfloat16)
    shape4 = (blocks, row_count // blocks, heads, HEAD_DIM)
    queries = projected[:, :width].reshape(shape4)
    key_rows = projected[:, width : 2 * width].reshape(shape4)
    value_rows = projected[:, 2 * width :].reshape(shape4)
    scores = (
        jnp.einsum("bqhd,bkhd->bhqk", queries, key_rows, preferred_element_type=jnp.float32)
        * scaling
    )
    same_session = segment[:, :, None] == segment[:, None, :]
    scores = jnp.where(same_session[:, None], scores, -1e30)
    row_peak = jnp.max(scores, axis=-1, keepdims=True)
    exponent = jnp.exp(scores - row_peak)
    probabilities = exponent / jnp.sum(exponent, axis=-1, keepdims=True)
    prob_rounded = probabilities.astype(jnp.bfloat16)
    attended = (
        jnp.einsum("bhqk,bkhd->bqhd", prob_rounded, value_rows, preferred_element_type=jnp.float32)
        .astype(jnp.bfloat16)
        .reshape(row_count, width)
    )
    return queries, key_rows, value_rows, probabilities, prob_rounded, attended


def attention_backward(forward, upstream, weights_qkv, weights_out):
    queries, key_rows, value_rows, probabilities, prob_rounded, _ = forward
    row_count = upstream.shape[0]
    width = weights_out.shape[1]
    scaling = HEAD_DIM ** (-0.5)
    grad_attended = jnp.dot(
        upstream, weights_out, preferred_element_type=jnp.float32
    ).astype(jnp.bfloat16)
    grad_heads = grad_attended.reshape(queries.shape)
    grad_prob = jnp.einsum(
        "bqhd,bkhd->bhqk", grad_heads, value_rows, preferred_element_type=jnp.float32
    )
    delta = jnp.sum(probabilities * grad_prob, axis=-1, keepdims=True)
    grad_score = (probabilities * (grad_prob - delta) * scaling).astype(jnp.bfloat16)
    grad_query = jnp.einsum(
        "bhqk,bkhd->bqhd", grad_score, key_rows, preferred_element_type=jnp.float32
    )
    grad_key = jnp.einsum(
        "bhqk,bqhd->bkhd", grad_score, queries, preferred_element_type=jnp.float32
    )
    grad_value = jnp.einsum(
        "bhqk,bqhd->bkhd", prob_rounded, grad_heads, preferred_element_type=jnp.float32
    )
    grad_qkv = jnp.concatenate(
        [
            grad_query.reshape(row_count, width),
            grad_key.reshape(row_count, width),
            grad_value.reshape(row_count, width),
        ],
        axis=1,
    ).astype(jnp.bfloat16)
    grad_normed = lax.dot_general(
        grad_qkv,
        weights_qkv,
        (((1,), (1,)), ((), ())),
        preferred_element_type=jnp.float32,
    )
    return grad_qkv, grad_normed


def embed_terms(embed_in_q, embed_out_q, aug_rows, grad_rows):
    pre = jnp.dot(embed_in_q.astype(jnp.float32), aug_rows, precision=lax.Precision.HIGHEST)
    hidden = gelu_value(pre).astype(jnp.bfloat16)
    term_out = jnp.dot(hidden, grad_rows, preferred_element_type=jnp.float32)
    grad_hidden = lax.dot_general(
        embed_out_q, grad_rows, (((1,), (1,)), ((), ())), preferred_element_type=jnp.float32
    )
    grad_pre = grad_hidden * gelu_slope(pre)
    term_in = lax.dot_general(
        grad_pre, aug_rows, (((1,), (1,)), ((), ())), precision=lax.Precision.HIGHEST
    )
    return (term_out, term_in)


def broadcast_from_first(block, axis):
    count = lax.axis_size(axis)
    index = lax.axis_index(axis)
    if count == 1:
        return block
    result = jnp.where(index == 0, block, lax.ppermute(block, axis, [(0, 1)]))
    if count > 2:
        back = lax.ppermute(block, axis, [(0, count - 1)])
        result = jnp.where(index == count - 1, back, result)
    if count <= 3:
        return result
    assert count == 4
    half = block.shape[0] // 2
    low = lax.ppermute(result[:half], axis, [(1, 2)])
    high = lax.ppermute(result[half:], axis, [(3, 2)])
    return jnp.where(index == 2, jnp.concatenate([low, high], axis=0), result)


def on_device(saved_inputs, attn_weights, grad_out, segments, coords, embed_in, embed_out):
    section_count = lax.axis_size("section")
    section_index = lax.axis_index("section")
    chip_count = lax.axis_size("xy")
    core = lax.axis_index("core")
    other = 1 - core
    micro_count = saved_inputs.shape[1]
    row_count = saved_inputs.shape[2]
    width = saved_inputs.shape[3]
    local_rows = attn_weights.shape[1]
    attn_width = attn_weights.shape[2] // 4
    half_width = attn_width // 2
    own_rows = micro_count * row_count
    embed_rows = embed_out.shape[0]

    mine = attn_weights[0].reshape(local_rows, 4, 2, half_width)
    given = swap_cores(pick(mine, other, 2))
    kept = pick(mine, core, 2)
    chip_rows = jnp.where(
        core == 0,
        jnp.concatenate([kept, given], axis=0),
        jnp.concatenate([given, kept], axis=0),
    ).reshape(2 * local_rows, 4 * half_width)
    weights_qkv = lax.all_gather(chip_rows[:, : 3 * half_width], "xy", axis=0, tiled=True)
    weights_qkv, out_rows = lax.optimization_barrier((weights_qkv, chip_rows[:, 3 * half_width :]))
    weights_out = lax.all_gather(out_rows, "xy", axis=0, tiled=True)

    embed_both = lax.all_gather(
        jnp.concatenate([embed_out, embed_in], axis=1), FSDP, axis=0, tiled=True
    )

    inputs_own = saved_inputs[0].reshape(own_rows, width)
    inputs_all = jnp.concatenate([inputs_own, swap_cores(inputs_own)], axis=0)
    segment_own = segments[:, 0, :]
    segment_all = jnp.concatenate([segment_own, swap_cores(segment_own)], axis=0)
    norm_scale_all, normed_all = normalize(inputs_all)
    norm_scale = norm_scale_all[:own_rows]
    values = inputs_own.astype(jnp.float32)
    forward = attention_forward(normed_all, weights_qkv, segment_all, 2 * micro_count)
    attended_all = forward[-1]

    top_grad = grad_out.reshape(own_rows, width)
    received = top_grad
    keep = None
    for step_index in range(section_count):
        active = section_count - 1 - step_index
        upstream = top_grad if step_index == 0 else received
        upstream_all = jnp.concatenate([upstream, swap_cores(upstream)], axis=0)
        grad_qkv, grad_normed = attention_backward(
            forward, upstream_all, weights_qkv, weights_out
        )
        grad_normed = grad_normed[:own_rows] + swap_cores(grad_normed[own_rows:])
        grad_inputs = (
            upstream.astype(jnp.float32)
            + norm_scale * grad_normed
            - values * norm_scale**3 * jnp.mean(values * grad_normed, axis=-1, keepdims=True)
        ).astype(jnp.bfloat16)
        fresh = (grad_qkv, upstream_all, grad_inputs)
        if keep is None:
            keep = fresh
        else:
            valid = section_index == active
            keep = tuple(jnp.where(valid, f, k) for f, k in zip(fresh, keep))
        if step_index < section_count - 1:
            pairs = [(i, i - 1) for i in range(1, section_count)]
            received = lax.ppermute(grad_inputs, "section", pairs)
    qkv_all, up_all, first_grad = keep
    first = lax.dot_general(
        normed_all, qkv_all, (((0,), (0,)), ((), ())), preferred_element_type=jnp.float32
    )
    second = lax.dot_general(
        up_all, attended_all, (((0,), (0,)), ((), ())), preferred_element_type=jnp.float32
    )
    grad_half = jnp.concatenate([first, second], axis=1).astype(jnp.bfloat16)
    chip_grad = lax.psum_scatter(grad_half, "xy", scatter_dimension=0, tiled=True)
    chip_grad = chip_grad.reshape(2, local_rows, 4, half_width)
    mine_grad = pick(chip_grad, core, 0)
    theirs_grad = swap_cores(pick(chip_grad, other, 0))
    attn_grad = jnp.where(
        core == 0,
        jnp.stack([mine_grad, theirs_grad], axis=2),
        jnp.stack([theirs_grad, mine_grad], axis=2),
    ).reshape(local_rows, 4 * attn_width).astype(jnp.float32)

    input_grad = broadcast_from_first(first_grad, "section")
    grad_all = jnp.concatenate([input_grad, swap_cores(input_grad)], axis=0)
    coords_own = coords.reshape(3, own_rows)
    coords_all = jnp.concatenate([coords_own, swap_cores(coords_own)], axis=1)
    augmented = jnp.concatenate(
        [coords_all, jnp.ones((1, 2 * own_rows), jnp.float32)], axis=0
    )
    embed_half = pick(
        embed_both.reshape(chip_count, 2, embed_rows, width + embed_in.shape[1]), core, 1
    ).reshape(chip_count * embed_rows, width + embed_in.shape[1])
    term_out, term_in = embed_terms(
        embed_half[:, width:], embed_half[:, :width], augmented, grad_all
    )
    terms = jnp.concatenate([term_out, term_in], axis=1).astype(jnp.bfloat16)
    pieces = lax.all_to_all(
        terms.reshape(chip_count, embed_rows, terms.shape[1]), "xy", 0, 0, tiled=False
    )
    summed = jnp.sum(pieces.astype(jnp.float32), axis=0)
    return (
        attn_grad[None],
        input_grad.reshape(micro_count, row_count, width),
        summed[:, :width],
        summed[:, width:],
    )


def solution(mesh):
    sections, fsdp = mesh.devices.shape
    inner = Mesh(mesh.devices.reshape(sections, fsdp // 2, 2), ("section", "xy", "core"))
    placed = (
        P("section", None, FSDP, None),
        P("section", FSDP, None),
        P(None, FSDP, None),
        P(None, FSDP, None),
        P(None, None, FSDP),
        P(("section",) + FSDP, None),
        P(("section",) + FSDP, None),
    )
    outer_specs = (
        P("section", "fsdp", None),
        P(None, "fsdp", None),
        P(("section", "fsdp"), None),
        P(("section", "fsdp"), None),
    )
    mapped = jax.shard_map(
        on_device,
        mesh=inner,
        in_specs=placed,
        out_specs=(
            P("section", FSDP, None),
            P(None, FSDP, None),
            P(("section",) + FSDP, None),
            P(("section",) + FSDP, None),
        ),
        check_vma=False,
    )

    def run(*args):
        outs = mapped(*args)
        return tuple(
            lax.with_sharding_constraint(o, NamedSharding(mesh, s))
            for o, s in zip(outs, outer_specs)
        )

    return run
```

```python
import jax
import jax.numpy as jnp
from jax import lax
from jax.sharding import Mesh, NamedSharding, PartitionSpec as P

HEAD_DIM = 64


EPS = 1e-05

FSDP = ("xy", "core")


def gelu_value(pre):
    return 0.5 * pre * (1.0 + jax.scipy.special.erf(pre / jnp.sqrt(2.0)))


def gelu_slope(pre):
    return 0.5 * (1.0 + jax.scipy.special.erf(pre / jnp.sqrt(2.0))) + pre * jnp.exp(
        -0.5 * pre * pre
    ) / jnp.sqrt(2.0 * jnp.pi)


def normalize(inputs):
    values = inputs.astype(jnp.float32)
    norm_scale = lax.rsqrt(jnp.mean(values * values, axis=-1, keepdims=True) + EPS)
    normed = (values * norm_scale).astype(jnp.bfloat16)
    return (norm_scale, normed)


def swap_cores(value):
    return lax.ppermute(value, "core", [(0, 1), (1, 0)])


def pick(value, index, axis):
    return lax.dynamic_index_in_dim(value, index, axis, keepdims=False)


def attention_forward(normed, weights_qkv, segment, blocks):
    row_count = normed.shape[0]
    width = weights_qkv.shape[1] // 3
    heads = width // HEAD_DIM
    scaling = HEAD_DIM ** (-0.5)
    projected = jnp.dot(
        normed, weights_qkv, preferred_element_type=jnp.float32
    ).astype(jnp.bfloat16)
    shape4 = (blocks, row_count // blocks, heads, HEAD_DIM)
    queries = projected[:, :width].reshape(shape4)
    key_rows = projected[:, width : 2 * width].reshape(shape4)
    value_rows = projected[:, 2 * width :].reshape(shape4)
    scores = (
        jnp.einsum("bqhd,bkhd->bhqk", queries, key_rows, preferred_element_type=jnp.float32)
        * scaling
    )
    same_session = segment[:, :, None] == segment[:, None, :]
    scores = jnp.where(same_session[:, None], scores, -1e30)
    row_peak = jnp.max(scores, axis=-1, keepdims=True)
    exponent = jnp.exp(scores - row_peak)
    probabilities = exponent / jnp.sum(exponent, axis=-1, keepdims=True)
    prob_rounded = probabilities.astype(jnp.bfloat16)
    attended = (
        jnp.einsum("bhqk,bkhd->bqhd", prob_rounded, value_rows, preferred_element_type=jnp.float32)
        .astype(jnp.bfloat16)
        .reshape(row_count, width)
    )
    return queries, key_rows, value_rows, probabilities, prob_rounded, attended


def attention_backward(forward, upstream, weights_qkv, weights_out):
    queries, key_rows, value_rows, probabilities, prob_rounded, _ = forward
    row_count = upstream.shape[0]
    width = weights_out.shape[1]
    scaling = HEAD_DIM ** (-0.5)
    grad_attended = jnp.dot(
        upstream, weights_out, preferred_element_type=jnp.float32
    ).astype(jnp.bfloat16)
    grad_heads = grad_attended.reshape(queries.shape)
    grad_prob = jnp.einsum(
        "bqhd,bkhd->bhqk", grad_heads, value_rows, preferred_element_type=jnp.float32
    )
    delta = jnp.sum(probabilities * grad_prob, axis=-1, keepdims=True)
    grad_score = (probabilities * (grad_prob - delta) * scaling).astype(jnp.bfloat16)
    grad_query = jnp.einsum(
        "bhqk,bkhd->bqhd", grad_score, key_rows, preferred_element_type=jnp.float32
    )
    grad_key = jnp.einsum(
        "bhqk,bqhd->bkhd", grad_score, queries, preferred_element_type=jnp.float32
    )
    grad_value = jnp.einsum(
        "bhqk,bqhd->bkhd", prob_rounded, grad_heads, preferred_element_type=jnp.float32
    )
    grad_qkv = jnp.concatenate(
        [
            grad_query.reshape(row_count, width),
            grad_key.reshape(row_count, width),
            grad_value.reshape(row_count, width),
        ],
        axis=1,
    ).astype(jnp.bfloat16)
    grad_normed = lax.dot_general(
        grad_qkv,
        weights_qkv,
        (((1,), (1,)), ((), ())),
        preferred_element_type=jnp.float32,
    )
    return grad_qkv, grad_normed


def embed_terms(embed_in_q, embed_out_q, aug_rows, grad_rows):
    pre = jnp.dot(embed_in_q.astype(jnp.float32), aug_rows, precision=lax.Precision.HIGHEST)
    hidden = gelu_value(pre).astype(jnp.bfloat16)
    term_out = jnp.dot(hidden, grad_rows, preferred_element_type=jnp.float32)
    grad_hidden = lax.dot_general(
        embed_out_q, grad_rows, (((1,), (1,)), ((), ())), preferred_element_type=jnp.float32
    )
    grad_pre = grad_hidden * gelu_slope(pre)
    term_in = lax.dot_general(
        grad_pre, aug_rows, (((1,), (1,)), ((), ())), precision=lax.Precision.HIGHEST
    )
    return (term_out, term_in)


def broadcast_from_first(block, axis):
    count = lax.axis_size(axis)
    index = lax.axis_index(axis)
    if count == 1:
        return block
    result = jnp.where(index == 0, block, lax.ppermute(block, axis, [(0, 1)]))
    if count > 2:
        back = lax.ppermute(block, axis, [(0, count - 1)])
        result = jnp.where(index == count - 1, back, result)
    if count <= 3:
        return result
    assert count == 4
    half = block.shape[0] // 2
    low = lax.ppermute(result[:half], axis, [(1, 2)])
    high = lax.ppermute(result[half:], axis, [(3, 2)])
    return jnp.where(index == 2, jnp.concatenate([low, high], axis=0), result)


def on_device(saved_inputs, attn_weights, grad_out, segments, coords, embed_in, embed_out):
    section_count = lax.axis_size("section")
    section_index = lax.axis_index("section")
    chip_count = lax.axis_size("xy")
    core = lax.axis_index("core")
    other = 1 - core
    micro_count = saved_inputs.shape[1]
    row_count = saved_inputs.shape[2]
    width = saved_inputs.shape[3]
    local_rows = attn_weights.shape[1]
    attn_width = attn_weights.shape[2] // 4
    half_width = attn_width // 2
    own_rows = micro_count * row_count
    embed_rows = embed_out.shape[0]

    mine = attn_weights[0].reshape(local_rows, 4, 2, half_width)
    given = swap_cores(pick(mine, other, 2))
    kept = pick(mine, core, 2)
    chip_rows = jnp.where(
        core == 0,
        jnp.concatenate([kept, given], axis=0),
        jnp.concatenate([given, kept], axis=0),
    ).reshape(2 * local_rows, 4 * half_width)
    layer = lax.all_to_all(
        jnp.broadcast_to(chip_rows[None], (chip_count,) + chip_rows.shape), "xy", 0, 0, tiled=False
    ).reshape(chip_count * chip_rows.shape[0], chip_rows.shape[1])
    weights_qkv = layer[:, : 3 * half_width]
    weights_out = layer[:, 3 * half_width :]

    embed_both = lax.all_gather(
        jnp.concatenate([embed_out, embed_in], axis=1), FSDP, axis=0, tiled=True
    )

    inputs_own = saved_inputs[0].reshape(own_rows, width)
    inputs_all = jnp.concatenate([inputs_own, swap_cores(inputs_own)], axis=0)
    segment_own = segments[:, 0, :]
    segment_all = jnp.concatenate([segment_own, swap_cores(segment_own)], axis=0)
    norm_scale_all, normed_all = normalize(inputs_all)
    norm_scale = norm_scale_all[:own_rows]
    values = inputs_own.astype(jnp.float32)
    forward = attention_forward(normed_all, weights_qkv, segment_all, 2 * micro_count)
    attended_all = forward[-1]

    top_grad = grad_out.reshape(own_rows, width)
    received = top_grad
    keep = None
    for step_index in range(section_count):
        active = section_count - 1 - step_index
        upstream = top_grad if step_index == 0 else received
        upstream_all = jnp.concatenate([upstream, swap_cores(upstream)], axis=0)
        grad_qkv, grad_normed = attention_backward(
            forward, upstream_all, weights_qkv, weights_out
        )
        grad_normed = grad_normed[:own_rows] + swap_cores(grad_normed[own_rows:])
        grad_inputs = (
            upstream.astype(jnp.float32)
            + norm_scale * grad_normed
            - values * norm_scale**3 * jnp.mean(values * grad_normed, axis=-1, keepdims=True)
        ).astype(jnp.bfloat16)
        fresh = (grad_qkv, upstream_all, grad_inputs)
        if keep is None:
            keep = fresh
        else:
            valid = section_index == active
            keep = tuple(jnp.where(valid, f, k) for f, k in zip(fresh, keep))
        if step_index < section_count - 1:
            pairs = [(i, i - 1) for i in range(1, section_count)]
            received = lax.ppermute(grad_inputs, "section", pairs)
    qkv_all, up_all, first_grad = keep
    first = lax.dot_general(
        normed_all, qkv_all, (((0,), (0,)), ((), ())), preferred_element_type=jnp.float32
    )
    second = lax.dot_general(
        up_all, attended_all, (((0,), (0,)), ((), ())), preferred_element_type=jnp.float32
    )
    grad_half = jnp.concatenate([first, second], axis=1).astype(jnp.bfloat16)
    chip_grad = jnp.sum(
        lax.all_to_all(
            grad_half.reshape(chip_count, 2 * local_rows, grad_half.shape[1]), "xy", 0, 0, tiled=False
        ).astype(jnp.float32),
        axis=0,
    )
    chip_grad = chip_grad.reshape(2, local_rows, 4, half_width)
    mine_grad = pick(chip_grad, core, 0)
    theirs_grad = swap_cores(pick(chip_grad, other, 0))
    attn_grad = jnp.where(
        core == 0,
        jnp.stack([mine_grad, theirs_grad], axis=2),
        jnp.stack([theirs_grad, mine_grad], axis=2),
    ).reshape(local_rows, 4 * attn_width)

    input_grad = broadcast_from_first(first_grad, "section")
    grad_all = jnp.concatenate([input_grad, swap_cores(input_grad)], axis=0)
    coords_own = coords.reshape(3, own_rows)
    coords_all = jnp.concatenate([coords_own, swap_cores(coords_own)], axis=1)
    augmented = jnp.concatenate(
        [coords_all, jnp.ones((1, 2 * own_rows), jnp.float32)], axis=0
    )
    embed_half = pick(
        embed_both.reshape(chip_count, 2, embed_rows, width + embed_in.shape[1]), core, 1
    ).reshape(chip_count * embed_rows, width + embed_in.shape[1])
    term_out, term_in = embed_terms(
        embed_half[:, width:], embed_half[:, :width], augmented, grad_all
    )
    terms = jnp.concatenate([term_out, term_in], axis=1).astype(jnp.bfloat16)
    pieces = lax.all_to_all(
        terms.reshape(chip_count, embed_rows, terms.shape[1]), "xy", 0, 0, tiled=False
    )
    summed = jnp.sum(pieces.astype(jnp.float32), axis=0)
    return (
        attn_grad[None],
        input_grad.reshape(micro_count, row_count, width),
        summed[:, :width],
        summed[:, width:],
    )


def solution(mesh):
    sections, fsdp = mesh.devices.shape
    inner = Mesh(mesh.devices.reshape(sections, fsdp // 2, 2), ("section", "xy", "core"))
    placed = (
        P("section", None, FSDP, None),
        P("section", FSDP, None),
        P(None, FSDP, None),
        P(None, FSDP, None),
        P(None, None, FSDP),
        P(("section",) + FSDP, None),
        P(("section",) + FSDP, None),
    )
    outer_specs = (
        P("section", "fsdp", None),
        P(None, "fsdp", None),
        P(("section", "fsdp"), None),
        P(("section", "fsdp"), None),
    )
    mapped = jax.shard_map(
        on_device,
        mesh=inner,
        in_specs=placed,
        out_specs=(
            P("section", FSDP, None),
            P(None, FSDP, None),
            P(("section",) + FSDP, None),
            P(("section",) + FSDP, None),
        ),
        check_vma=False,
    )

    def run(*args):
        outs = mapped(*args)
        return tuple(
            lax.with_sharding_constraint(o, NamedSharding(mesh, s))
            for o, s in zip(outs, outer_specs)
        )

    return run
```

```python
import jax
import jax.numpy as jnp
from jax import lax
from jax.sharding import Mesh, NamedSharding, PartitionSpec as P

HEAD_DIM = 64


EPS = 1e-05

FSDP = ("xy", "core")


def gelu_value(pre):
    return 0.5 * pre * (1.0 + jax.scipy.special.erf(pre / jnp.sqrt(2.0)))


def gelu_slope(pre):
    return 0.5 * (1.0 + jax.scipy.special.erf(pre / jnp.sqrt(2.0))) + pre * jnp.exp(
        -0.5 * pre * pre
    ) / jnp.sqrt(2.0 * jnp.pi)


def normalize(inputs):
    values = inputs.astype(jnp.float32)
    norm_scale = lax.rsqrt(jnp.mean(values * values, axis=-1, keepdims=True) + EPS)
    normed = (values * norm_scale).astype(jnp.bfloat16)
    return (norm_scale, normed)


def swap_cores(value):
    return lax.ppermute(value, "core", [(0, 1), (1, 0)])


def pick(value, index, axis):
    return lax.dynamic_index_in_dim(value, index, axis, keepdims=False)


def attention_forward(normed, weights_qkv, segment, blocks):
    row_count = normed.shape[0]
    width = weights_qkv.shape[1] // 3
    heads = width // HEAD_DIM
    scaling = HEAD_DIM ** (-0.5)
    projected = jnp.dot(
        normed, weights_qkv, preferred_element_type=jnp.float32
    ).astype(jnp.bfloat16)
    shape4 = (blocks, row_count // blocks, heads, HEAD_DIM)
    queries = projected[:, :width].reshape(shape4)
    key_rows = projected[:, width : 2 * width].reshape(shape4)
    value_rows = projected[:, 2 * width :].reshape(shape4)
    scores = (
        jnp.einsum("bqhd,bkhd->bhqk", queries, key_rows, preferred_element_type=jnp.float32)
        * scaling
    )
    same_session = segment[:, :, None] == segment[:, None, :]
    scores = jnp.where(same_session[:, None], scores, -1e30)
    row_peak = jnp.max(scores, axis=-1, keepdims=True)
    exponent = jnp.exp(scores - row_peak)
    probabilities = exponent / jnp.sum(exponent, axis=-1, keepdims=True)
    prob_rounded = probabilities.astype(jnp.bfloat16)
    attended = (
        jnp.einsum("bhqk,bkhd->bqhd", prob_rounded, value_rows, preferred_element_type=jnp.float32)
        .astype(jnp.bfloat16)
        .reshape(row_count, width)
    )
    return queries, key_rows, value_rows, probabilities, prob_rounded, attended


def attention_backward(forward, upstream, weights_qkv, weights_out):
    queries, key_rows, value_rows, probabilities, prob_rounded, _ = forward
    row_count = upstream.shape[0]
    width = weights_out.shape[1]
    scaling = HEAD_DIM ** (-0.5)
    grad_attended = jnp.dot(
        upstream, weights_out, preferred_element_type=jnp.float32
    ).astype(jnp.bfloat16)
    grad_heads = grad_attended.reshape(queries.shape)
    grad_prob = jnp.einsum(
        "bqhd,bkhd->bhqk", grad_heads, value_rows, preferred_element_type=jnp.float32
    )
    delta = jnp.sum(probabilities * grad_prob, axis=-1, keepdims=True)
    grad_score = (probabilities * (grad_prob - delta) * scaling).astype(jnp.bfloat16)
    grad_query = jnp.einsum(
        "bhqk,bkhd->bqhd", grad_score, key_rows, preferred_element_type=jnp.float32
    )
    grad_key = jnp.einsum(
        "bhqk,bqhd->bkhd", grad_score, queries, preferred_element_type=jnp.float32
    )
    grad_value = jnp.einsum(
        "bhqk,bqhd->bkhd", prob_rounded, grad_heads, preferred_element_type=jnp.float32
    )
    grad_qkv = jnp.concatenate(
        [
            grad_query.reshape(row_count, width),
            grad_key.reshape(row_count, width),
            grad_value.reshape(row_count, width),
        ],
        axis=1,
    ).astype(jnp.bfloat16)
    grad_normed = lax.dot_general(
        grad_qkv,
        weights_qkv,
        (((1,), (1,)), ((), ())),
        preferred_element_type=jnp.float32,
    )
    return grad_qkv, grad_normed


def embed_terms(embed_in_q, embed_out_q, aug_rows, grad_rows):
    pre = jnp.dot(embed_in_q.astype(jnp.float32), aug_rows, precision=lax.Precision.HIGHEST)
    hidden = gelu_value(pre).astype(jnp.bfloat16)
    term_out = jnp.dot(hidden, grad_rows, preferred_element_type=jnp.float32)
    grad_hidden = lax.dot_general(
        embed_out_q, grad_rows, (((1,), (1,)), ((), ())), preferred_element_type=jnp.float32
    )
    grad_pre = grad_hidden * gelu_slope(pre)
    term_in = lax.dot_general(
        grad_pre, aug_rows, (((1,), (1,)), ((), ())), precision=lax.Precision.HIGHEST
    )
    return (term_out, term_in)


def broadcast_from_first(block, axis):
    count = lax.axis_size(axis)
    index = lax.axis_index(axis)
    if count == 1:
        return block
    result = jnp.where(index == 0, block, lax.ppermute(block, axis, [(0, 1)]))
    if count > 2:
        back = lax.ppermute(block, axis, [(0, count - 1)])
        result = jnp.where(index == count - 1, back, result)
    if count <= 3:
        return result
    assert count == 4
    half = block.shape[0] // 2
    low = lax.ppermute(result[:half], axis, [(1, 2)])
    high = lax.ppermute(result[half:], axis, [(3, 2)])
    return jnp.where(index == 2, jnp.concatenate([low, high], axis=0), result)


def on_device(saved_inputs, attn_weights, grad_out, segments, coords, embed_in, embed_out):
    section_count = lax.axis_size("section")
    section_index = lax.axis_index("section")
    chip_count = lax.axis_size("xy")
    core = lax.axis_index("core")
    other = 1 - core
    micro_count = saved_inputs.shape[1]
    row_count = saved_inputs.shape[2]
    width = saved_inputs.shape[3]
    local_rows = attn_weights.shape[1]
    attn_width = attn_weights.shape[2] // 4
    half_width = attn_width // 2
    own_rows = micro_count * row_count
    embed_rows = embed_out.shape[0]

    mine = attn_weights[0].reshape(local_rows, 4, 2, half_width)
    given = swap_cores(pick(mine, other, 2))
    kept = pick(mine, core, 2)
    chip_rows = jnp.where(
        core == 0,
        jnp.concatenate([kept, given], axis=0),
        jnp.concatenate([given, kept], axis=0),
    ).reshape(2 * local_rows, 4 * half_width)
    layer = lax.all_gather(chip_rows, "xy", axis=0, tiled=True)
    weights_qkv = layer[:, : 3 * half_width]
    weights_out = layer[:, 3 * half_width :]

    embed_both = lax.all_gather(
        jnp.concatenate([embed_out, embed_in], axis=1), FSDP, axis=0, tiled=True
    )

    inputs_own = saved_inputs[0].reshape(own_rows, width)
    inputs_all = jnp.concatenate([inputs_own, swap_cores(inputs_own)], axis=0)
    segment_own = segments[:, 0, :]
    segment_all = jnp.concatenate([segment_own, swap_cores(segment_own)], axis=0)
    norm_scale_all, normed_all = normalize(inputs_all)
    norm_scale = norm_scale_all[:own_rows]
    values = inputs_own.astype(jnp.float32)
    forward = attention_forward(normed_all, weights_qkv, segment_all, 2 * micro_count)
    attended_all = forward[-1]

    top_grad = grad_out.reshape(own_rows, width)
    received = top_grad
    keep = None
    for step_index in range(section_count):
        active = section_count - 1 - step_index
        upstream = top_grad if step_index == 0 else received
        upstream_all = jnp.concatenate([upstream, swap_cores(upstream)], axis=0)
        grad_qkv, grad_normed = attention_backward(
            forward, upstream_all, weights_qkv, weights_out
        )
        grad_normed = grad_normed[:own_rows] + swap_cores(grad_normed[own_rows:])
        grad_inputs = (
            upstream.astype(jnp.float32)
            + norm_scale * grad_normed
            - values * norm_scale**3 * jnp.mean(values * grad_normed, axis=-1, keepdims=True)
        ).astype(jnp.bfloat16)
        fresh = (grad_qkv, upstream_all, grad_inputs)
        if keep is None:
            keep = fresh
        else:
            valid = section_index == active
            keep = tuple(jnp.where(valid, f, k) for f, k in zip(fresh, keep))
        if step_index < section_count - 1:
            pairs = [(i, i - 1) for i in range(1, section_count)]
            received = lax.ppermute(grad_inputs, "section", pairs)
    qkv_all, up_all, first_grad = keep
    chip_tokens = qkv_all.shape[0]
    left = lax.optimization_barrier(jnp.concatenate([normed_all, up_all], axis=0).T)
    right = jnp.concatenate(
        [
            jnp.concatenate(
                [qkv_all, jnp.zeros((chip_tokens, half_width), qkv_all.dtype)], axis=1
            ),
            jnp.concatenate(
                [jnp.zeros((chip_tokens, 3 * half_width), qkv_all.dtype), attended_all], axis=1
            ),
        ],
        axis=0,
    )
    grad_half = jnp.dot(left, right, preferred_element_type=jnp.float32).astype(jnp.bfloat16)
    chip_grad = lax.psum_scatter(grad_half, "xy", scatter_dimension=0, tiled=True)
    chip_grad = chip_grad.reshape(2, local_rows, 4, half_width)
    mine_grad = pick(chip_grad, core, 0)
    theirs_grad = swap_cores(pick(chip_grad, other, 0))
    attn_grad = jnp.where(
        core == 0,
        jnp.stack([mine_grad, theirs_grad], axis=2),
        jnp.stack([theirs_grad, mine_grad], axis=2),
    ).reshape(local_rows, 4 * attn_width).astype(jnp.float32)

    input_grad = broadcast_from_first(first_grad, "section")
    grad_all = jnp.concatenate([input_grad, swap_cores(input_grad)], axis=0)
    coords_own = coords.reshape(3, own_rows)
    coords_all = jnp.concatenate([coords_own, swap_cores(coords_own)], axis=1)
    augmented = jnp.concatenate(
        [coords_all, jnp.ones((1, 2 * own_rows), jnp.float32)], axis=0
    )
    embed_half = pick(
        embed_both.reshape(chip_count, 2, embed_rows, width + embed_in.shape[1]), core, 1
    ).reshape(chip_count * embed_rows, width + embed_in.shape[1])
    term_out, term_in = embed_terms(
        embed_half[:, width:], embed_half[:, :width], augmented, grad_all
    )
    terms = jnp.concatenate([term_out, term_in], axis=1).astype(jnp.bfloat16)
    pieces = lax.all_to_all(
        terms.reshape(chip_count, embed_rows, terms.shape[1]), "xy", 0, 0, tiled=False
    )
    summed = jnp.sum(pieces.astype(jnp.float32), axis=0)
    return (
        attn_grad[None],
        input_grad.reshape(micro_count, row_count, width),
        summed[:, :width],
        summed[:, width:],
    )


def solution(mesh):
    sections, fsdp = mesh.devices.shape
    inner = Mesh(mesh.devices.reshape(sections, fsdp // 2, 2), ("section", "xy", "core"))
    placed = (
        P("section", None, FSDP, None),
        P("section", FSDP, None),
        P(None, FSDP, None),
        P(None, FSDP, None),
        P(None, None, FSDP),
        P(("section",) + FSDP, None),
        P(("section",) + FSDP, None),
    )
    outer_specs = (
        P("section", "fsdp", None),
        P(None, "fsdp", None),
        P(("section", "fsdp"), None),
        P(("section", "fsdp"), None),
    )
    mapped = jax.shard_map(
        on_device,
        mesh=inner,
        in_specs=placed,
        out_specs=(
            P("section", FSDP, None),
            P(None, FSDP, None),
            P(("section",) + FSDP, None),
            P(("section",) + FSDP, None),
        ),
        check_vma=False,
    )

    def run(*args):
        outs = mapped(*args)
        return tuple(
            lax.with_sharding_constraint(o, NamedSharding(mesh, s))
            for o, s in zip(outs, outer_specs)
        )

    return run
```

```python
import jax
import jax.numpy as jnp
from jax import lax
from jax.sharding import Mesh, NamedSharding, PartitionSpec as P

HEAD_DIM = 64


EPS = 1e-05

FSDP = ("xy", "core")


def gelu_value(pre):
    return 0.5 * pre * (1.0 + jax.scipy.special.erf(pre / jnp.sqrt(2.0)))


def gelu_slope(pre):
    return 0.5 * (1.0 + jax.scipy.special.erf(pre / jnp.sqrt(2.0))) + pre * jnp.exp(
        -0.5 * pre * pre
    ) / jnp.sqrt(2.0 * jnp.pi)


def normalize(inputs):
    values = inputs.astype(jnp.float32)
    norm_scale = lax.rsqrt(jnp.mean(values * values, axis=-1, keepdims=True) + EPS)
    normed = (values * norm_scale).astype(jnp.bfloat16)
    return (norm_scale, normed)


def swap_cores(value):
    return lax.ppermute(value, "core", [(0, 1), (1, 0)])


def pick(value, index, axis):
    return lax.dynamic_index_in_dim(value, index, axis, keepdims=False)


def attention_forward(normed, weights_qkv, segment, blocks):
    row_count = normed.shape[0]
    width = weights_qkv.shape[1] // 3
    heads = width // HEAD_DIM
    scaling = HEAD_DIM ** (-0.5)
    projected = jnp.dot(
        normed, weights_qkv, preferred_element_type=jnp.float32
    ).astype(jnp.bfloat16)
    shape3 = (row_count, heads, HEAD_DIM)
    queries = projected[:, :width].reshape(shape3)
    key_rows = projected[:, width : 2 * width].reshape(shape3)
    value_rows = projected[:, 2 * width :].reshape(shape3)
    scores = (
        jnp.einsum("qhd,khd->hqk", queries, key_rows, preferred_element_type=jnp.float32)
        * scaling
    )
    block_of = jnp.arange(row_count) // (row_count // blocks)
    flat = segment.reshape(row_count)
    same_session = (flat[:, None] == flat[None, :]) & (block_of[:, None] == block_of[None, :])
    scores = jnp.where(same_session[None], scores, -1e30)
    row_peak = jnp.max(scores, axis=-1, keepdims=True)
    exponent = jnp.exp(scores - row_peak)
    probabilities = exponent / jnp.sum(exponent, axis=-1, keepdims=True)
    prob_rounded = probabilities.astype(jnp.bfloat16)
    attended = (
        jnp.einsum("hqk,khd->qhd", prob_rounded, value_rows, preferred_element_type=jnp.float32)
        .astype(jnp.bfloat16)
        .reshape(row_count, width)
    )
    return queries, key_rows, value_rows, probabilities, prob_rounded, attended


def attention_backward(forward, upstream, weights_qkv, weights_out):
    queries, key_rows, value_rows, probabilities, prob_rounded, _ = forward
    row_count = upstream.shape[0]
    width = weights_out.shape[1]
    scaling = HEAD_DIM ** (-0.5)
    grad_attended = jnp.dot(
        upstream, weights_out, preferred_element_type=jnp.float32
    ).astype(jnp.bfloat16)
    grad_heads = grad_attended.reshape(queries.shape)
    grad_prob = jnp.einsum(
        "qhd,khd->hqk", grad_heads, value_rows, preferred_element_type=jnp.float32
    )
    delta = jnp.sum(probabilities * grad_prob, axis=-1, keepdims=True)
    grad_score = (probabilities * (grad_prob - delta) * scaling).astype(jnp.bfloat16)
    grad_query = jnp.einsum(
        "hqk,khd->qhd", grad_score, key_rows, preferred_element_type=jnp.float32
    )
    grad_key = jnp.einsum(
        "hqk,qhd->khd", grad_score, queries, preferred_element_type=jnp.float32
    )
    grad_value = jnp.einsum(
        "hqk,qhd->khd", prob_rounded, grad_heads, preferred_element_type=jnp.float32
    )
    grad_qkv = jnp.concatenate(
        [
            grad_query.reshape(row_count, width),
            grad_key.reshape(row_count, width),
            grad_value.reshape(row_count, width),
        ],
        axis=1,
    ).astype(jnp.bfloat16)
    grad_normed = lax.dot_general(
        grad_qkv,
        weights_qkv,
        (((1,), (1,)), ((), ())),
        preferred_element_type=jnp.float32,
    )
    return grad_qkv, grad_normed


def embed_terms(embed_in_q, embed_out_q, aug_rows, grad_rows):
    pre = jnp.dot(embed_in_q.astype(jnp.float32), aug_rows, precision=lax.Precision.HIGHEST)
    hidden = gelu_value(pre).astype(jnp.bfloat16)
    term_out = jnp.dot(hidden, grad_rows, preferred_element_type=jnp.float32)
    grad_hidden = lax.dot_general(
        embed_out_q, grad_rows, (((1,), (1,)), ((), ())), preferred_element_type=jnp.float32
    )
    grad_pre = grad_hidden * gelu_slope(pre)
    term_in = lax.dot_general(
        grad_pre, aug_rows, (((1,), (1,)), ((), ())), precision=lax.Precision.HIGHEST
    )
    return (term_out, term_in)


def broadcast_from_first(block, axis):
    count = lax.axis_size(axis)
    index = lax.axis_index(axis)
    if count == 1:
        return block
    result = jnp.where(index == 0, block, lax.ppermute(block, axis, [(0, 1)]))
    if count > 2:
        back = lax.ppermute(block, axis, [(0, count - 1)])
        result = jnp.where(index == count - 1, back, result)
    if count <= 3:
        return result
    assert count == 4
    half = block.shape[0] // 2
    low = lax.ppermute(result[:half], axis, [(1, 2)])
    high = lax.ppermute(result[half:], axis, [(3, 2)])
    return jnp.where(index == 2, jnp.concatenate([low, high], axis=0), result)


def on_device(saved_inputs, attn_weights, grad_out, segments, coords, embed_in, embed_out):
    section_count = lax.axis_size("section")
    section_index = lax.axis_index("section")
    chip_count = lax.axis_size("xy")
    core = lax.axis_index("core")
    other = 1 - core
    micro_count = saved_inputs.shape[1]
    row_count = saved_inputs.shape[2]
    width = saved_inputs.shape[3]
    local_rows = attn_weights.shape[1]
    attn_width = attn_weights.shape[2] // 4
    half_width = attn_width // 2
    own_rows = micro_count * row_count
    embed_rows = embed_out.shape[0]

    mine = attn_weights[0].reshape(local_rows, 4, 2, half_width)
    given = swap_cores(pick(mine, other, 2))
    kept = pick(mine, core, 2)
    chip_rows = jnp.where(
        core == 0,
        jnp.concatenate([kept, given], axis=0),
        jnp.concatenate([given, kept], axis=0),
    ).reshape(2 * local_rows, 4 * half_width)
    layer = lax.all_gather(chip_rows, "xy", axis=0, tiled=True)
    weights_qkv = layer[:, : 3 * half_width]
    weights_out = layer[:, 3 * half_width :]

    embed_both = lax.all_gather(
        jnp.concatenate([embed_out, embed_in], axis=1), FSDP, axis=0, tiled=True
    )

    inputs_own = saved_inputs[0].reshape(own_rows, width)
    inputs_all = jnp.concatenate([inputs_own, swap_cores(inputs_own)], axis=0)
    segment_own = segments[:, 0, :]
    segment_all = jnp.concatenate([segment_own, swap_cores(segment_own)], axis=0)
    norm_scale_all, normed_all = normalize(inputs_all)
    norm_scale = norm_scale_all[:own_rows]
    values = inputs_own.astype(jnp.float32)
    forward = attention_forward(normed_all, weights_qkv, segment_all, 2 * micro_count)
    attended_all = forward[-1]

    top_grad = grad_out.reshape(own_rows, width)
    received = top_grad
    keep = None
    for step_index in range(section_count):
        active = section_count - 1 - step_index
        upstream = top_grad if step_index == 0 else received
        upstream_all = jnp.concatenate([upstream, swap_cores(upstream)], axis=0)
        grad_qkv, grad_normed = attention_backward(
            forward, upstream_all, weights_qkv, weights_out
        )
        grad_normed = grad_normed[:own_rows] + swap_cores(grad_normed[own_rows:])
        grad_inputs = (
            upstream.astype(jnp.float32)
            + norm_scale * grad_normed
            - values * norm_scale**3 * jnp.mean(values * grad_normed, axis=-1, keepdims=True)
        ).astype(jnp.bfloat16)
        fresh = (grad_qkv, upstream_all, grad_inputs)
        if keep is None:
            keep = fresh
        else:
            valid = section_index == active
            keep = tuple(jnp.where(valid, f, k) for f, k in zip(fresh, keep))
        if step_index < section_count - 1:
            pairs = [(i, i - 1) for i in range(1, section_count)]
            received = lax.ppermute(grad_inputs, "section", pairs)
    qkv_all, up_all, first_grad = keep
    chip_tokens = qkv_all.shape[0]
    left = lax.optimization_barrier(jnp.concatenate([normed_all, up_all], axis=0).T)
    right = jnp.concatenate(
        [
            jnp.concatenate(
                [qkv_all, jnp.zeros((chip_tokens, half_width), qkv_all.dtype)], axis=1
            ),
            jnp.concatenate(
                [jnp.zeros((chip_tokens, 3 * half_width), qkv_all.dtype), attended_all], axis=1
            ),
        ],
        axis=0,
    )
    grad_half = jnp.dot(left, right, preferred_element_type=jnp.float32).astype(jnp.bfloat16)
    chip_grad = lax.psum_scatter(grad_half, "xy", scatter_dimension=0, tiled=True)
    chip_grad = chip_grad.reshape(2, local_rows, 4, half_width)
    mine_grad = pick(chip_grad, core, 0)
    theirs_grad = swap_cores(pick(chip_grad, other, 0))
    attn_grad = jnp.where(
        core == 0,
        jnp.stack([mine_grad, theirs_grad], axis=2),
        jnp.stack([theirs_grad, mine_grad], axis=2),
    ).reshape(local_rows, 4 * attn_width).astype(jnp.float32)

    input_grad = broadcast_from_first(first_grad, "section")
    grad_all = jnp.concatenate([input_grad, swap_cores(input_grad)], axis=0)
    coords_own = coords.reshape(3, own_rows)
    coords_all = jnp.concatenate([coords_own, swap_cores(coords_own)], axis=1)
    augmented = jnp.concatenate(
        [coords_all, jnp.ones((1, 2 * own_rows), jnp.float32)], axis=0
    )
    embed_half = pick(
        embed_both.reshape(chip_count, 2, embed_rows, width + embed_in.shape[1]), core, 1
    ).reshape(chip_count * embed_rows, width + embed_in.shape[1])
    term_out, term_in = embed_terms(
        embed_half[:, width:], embed_half[:, :width], augmented, grad_all
    )
    terms = jnp.concatenate([term_out, term_in], axis=1).astype(jnp.bfloat16)
    pieces = lax.all_to_all(
        terms.reshape(chip_count, embed_rows, terms.shape[1]), "xy", 0, 0, tiled=False
    )
    summed = jnp.sum(pieces.astype(jnp.float32), axis=0)
    return (
        attn_grad[None],
        input_grad.reshape(micro_count, row_count, width),
        summed[:, :width],
        summed[:, width:],
    )


def solution(mesh):
    sections, fsdp = mesh.devices.shape
    inner = Mesh(mesh.devices.reshape(sections, fsdp // 2, 2), ("section", "xy", "core"))
    placed = (
        P("section", None, FSDP, None),
        P("section", FSDP, None),
        P(None, FSDP, None),
        P(None, FSDP, None),
        P(None, None, FSDP),
        P(("section",) + FSDP, None),
        P(("section",) + FSDP, None),
    )
    outer_specs = (
        P("section", "fsdp", None),
        P(None, "fsdp", None),
        P(("section", "fsdp"), None),
        P(("section", "fsdp"), None),
    )
    mapped = jax.shard_map(
        on_device,
        mesh=inner,
        in_specs=placed,
        out_specs=(
            P("section", FSDP, None),
            P(None, FSDP, None),
            P(("section",) + FSDP, None),
            P(("section",) + FSDP, None),
        ),
        check_vma=False,
    )

    def run(*args):
        outs = mapped(*args)
        return tuple(
            lax.with_sharding_constraint(o, NamedSharding(mesh, s))
            for o, s in zip(outs, outer_specs)
        )

    return run
```

```python
import jax
import jax.numpy as jnp
from jax import lax
from jax.sharding import Mesh, NamedSharding, PartitionSpec as P

HEAD_DIM = 64


EPS = 1e-05

FSDP = ("xy", "core")


def gelu_value(pre):
    return 0.5 * pre * (1.0 + jax.scipy.special.erf(pre / jnp.sqrt(2.0)))


def gelu_slope(pre):
    return 0.5 * (1.0 + jax.scipy.special.erf(pre / jnp.sqrt(2.0))) + pre * jnp.exp(
        -0.5 * pre * pre
    ) / jnp.sqrt(2.0 * jnp.pi)


def normalize(inputs):
    values = inputs.astype(jnp.float32)
    norm_scale = lax.rsqrt(jnp.mean(values * values, axis=-1, keepdims=True) + EPS)
    normed = (values * norm_scale).astype(jnp.bfloat16)
    return (norm_scale, normed)


def swap_cores(value):
    return lax.ppermute(value, "core", [(0, 1), (1, 0)])


def pick(value, index, axis):
    return lax.dynamic_index_in_dim(value, index, axis, keepdims=False)


def attention_forward(normed, weights_qkv, segment, blocks):
    row_count = normed.shape[0]
    width = weights_qkv.shape[1] // 3
    heads = width // HEAD_DIM
    scaling = HEAD_DIM ** (-0.5)
    projected = jnp.dot(
        normed, weights_qkv, preferred_element_type=jnp.float32
    ).astype(jnp.bfloat16)
    shape4 = (blocks, row_count // blocks, heads, HEAD_DIM)
    queries = projected[:, :width].reshape(shape4)
    key_rows = projected[:, width : 2 * width].reshape(shape4)
    value_rows = projected[:, 2 * width :].reshape(shape4)
    scores = (
        jnp.einsum("bqhd,bkhd->bhqk", queries, key_rows, preferred_element_type=jnp.float32)
        * scaling
    )
    same_session = segment[:, :, None] == segment[:, None, :]
    scores = jnp.where(same_session[:, None], scores, -1e30)
    row_peak = jnp.max(scores, axis=-1, keepdims=True)
    exponent = jnp.exp(scores - row_peak)
    probabilities = exponent / jnp.sum(exponent, axis=-1, keepdims=True)
    prob_rounded = probabilities.astype(jnp.bfloat16)
    attended = (
        jnp.einsum("bhqk,bkhd->bqhd", prob_rounded, value_rows, preferred_element_type=jnp.float32)
        .astype(jnp.bfloat16)
        .reshape(row_count, width)
    )
    return queries, key_rows, value_rows, probabilities, prob_rounded, attended


def attention_backward(forward, upstream, weights_qkv, weights_out):
    queries, key_rows, value_rows, probabilities, prob_rounded, _ = forward
    row_count = upstream.shape[0]
    width = weights_out.shape[1]
    scaling = HEAD_DIM ** (-0.5)
    grad_attended = jnp.dot(
        upstream, weights_out, preferred_element_type=jnp.float32
    ).astype(jnp.bfloat16)
    grad_heads = grad_attended.reshape(queries.shape)
    grad_prob = jnp.einsum(
        "bqhd,bkhd->bhqk", grad_heads, value_rows, preferred_element_type=jnp.float32
    )
    delta = jnp.sum(probabilities * grad_prob, axis=-1, keepdims=True)
    grad_score = (probabilities * (grad_prob - delta) * scaling).astype(jnp.bfloat16)
    grad_query = jnp.einsum(
        "bhqk,bkhd->bqhd", grad_score, key_rows, preferred_element_type=jnp.float32
    )
    grad_key = jnp.einsum(
        "bhqk,bqhd->bkhd", grad_score, queries, preferred_element_type=jnp.float32
    )
    grad_value = jnp.einsum(
        "bhqk,bqhd->bkhd", prob_rounded, grad_heads, preferred_element_type=jnp.float32
    )
    grad_qkv = jnp.concatenate(
        [
            grad_query.reshape(row_count, width),
            grad_key.reshape(row_count, width),
            grad_value.reshape(row_count, width),
        ],
        axis=1,
    ).astype(jnp.bfloat16)
    return grad_qkv


def normed_grad(grad_qkv, weights_qkv):
    return lax.dot_general(
        grad_qkv,
        weights_qkv,
        (((1,), (1,)), ((), ())),
        preferred_element_type=jnp.float32,
    )


def embed_terms(embed_in_q, embed_out_q, aug_rows, grad_rows):
    pre = jnp.dot(embed_in_q.astype(jnp.float32), aug_rows, precision=lax.Precision.HIGHEST)
    hidden = gelu_value(pre).astype(jnp.bfloat16)
    term_out = jnp.dot(hidden, grad_rows, preferred_element_type=jnp.float32)
    grad_hidden = lax.dot_general(
        embed_out_q, grad_rows, (((1,), (1,)), ((), ())), preferred_element_type=jnp.float32
    )
    grad_pre = grad_hidden * gelu_slope(pre)
    term_in = lax.dot_general(
        grad_pre, aug_rows, (((1,), (1,)), ((), ())), precision=lax.Precision.HIGHEST
    )
    return (term_out, term_in)


def broadcast_from_first(block, axis):
    count = lax.axis_size(axis)
    index = lax.axis_index(axis)
    if count == 1:
        return block
    result = jnp.where(index == 0, block, lax.ppermute(block, axis, [(0, 1)]))
    if count > 2:
        back = lax.ppermute(block, axis, [(0, count - 1)])
        result = jnp.where(index == count - 1, back, result)
    if count <= 3:
        return result
    assert count == 4
    half = block.shape[0] // 2
    low = lax.ppermute(result[:half], axis, [(1, 2)])
    high = lax.ppermute(result[half:], axis, [(3, 2)])
    return jnp.where(index == 2, jnp.concatenate([low, high], axis=0), result)


def on_device(saved_inputs, attn_weights, grad_out, segments, coords, embed_in, embed_out):
    section_count = lax.axis_size("section")
    section_index = lax.axis_index("section")
    chip_count = lax.axis_size("xy")
    core = lax.axis_index("core")
    other = 1 - core
    micro_count = saved_inputs.shape[1]
    row_count = saved_inputs.shape[2]
    width = saved_inputs.shape[3]
    local_rows = attn_weights.shape[1]
    attn_width = attn_weights.shape[2] // 4
    half_width = attn_width // 2
    own_rows = micro_count * row_count
    embed_rows = embed_out.shape[0]

    mine = attn_weights[0].reshape(local_rows, 4, 2, half_width)
    given = swap_cores(pick(mine, other, 2))
    kept = pick(mine, core, 2)
    chip_rows = jnp.where(
        core == 0,
        jnp.concatenate([kept, given], axis=0),
        jnp.concatenate([given, kept], axis=0),
    ).reshape(2 * local_rows, 4 * half_width)
    layer = lax.all_gather(chip_rows, "xy", axis=0, tiled=True)
    weights_qkv = layer[:, : 3 * half_width]
    weights_out = layer[:, 3 * half_width :]

    embed_both = lax.all_gather(
        jnp.concatenate([embed_out, embed_in], axis=1), FSDP, axis=0, tiled=True
    )

    inputs_own = saved_inputs[0].reshape(own_rows, width)
    inputs_all = jnp.concatenate([inputs_own, swap_cores(inputs_own)], axis=0)
    segment_own = segments[:, 0, :]
    segment_all = jnp.concatenate([segment_own, swap_cores(segment_own)], axis=0)
    norm_scale_all, normed_all = normalize(inputs_all)
    norm_scale = norm_scale_all[:own_rows]
    values = inputs_own.astype(jnp.float32)
    forward = attention_forward(normed_all, weights_qkv, segment_all, 2 * micro_count)
    attended_all = forward[-1]

    top_grad = grad_out.reshape(own_rows, width)
    received = top_grad
    keep = None
    keep_grad = None
    chip_tokens = 2 * own_rows
    for step_index in range(section_count):
        active = section_count - 1 - step_index
        upstream = top_grad if step_index == 0 else received
        upstream_all = jnp.concatenate([upstream, swap_cores(upstream)], axis=0)
        grad_qkv = attention_backward(forward, upstream_all, weights_qkv, weights_out)
        fresh = (grad_qkv, upstream_all)
        if keep is None:
            keep = fresh
        else:
            valid = section_index == active
            keep = tuple(jnp.where(valid, f, k) for f, k in zip(fresh, keep))
        if step_index == section_count - 1:
            qkv_all, up_all = keep
            left = jnp.concatenate([normed_all, up_all], axis=0).T
            right = jnp.concatenate(
                [
                    jnp.concatenate(
                        [qkv_all, jnp.zeros((chip_tokens, half_width), qkv_all.dtype)], axis=1
                    ),
                    jnp.concatenate(
                        [jnp.zeros((chip_tokens, 3 * half_width), qkv_all.dtype), attended_all],
                        axis=1,
                    ),
                ],
                axis=0,
            )
            grad_half = jnp.dot(left, right, preferred_element_type=jnp.float32).astype(
                jnp.bfloat16
            )
            grad_half, grad_qkv = lax.optimization_barrier((grad_half, grad_qkv))
        grad_normed = normed_grad(grad_qkv, weights_qkv)
        grad_normed = grad_normed[:own_rows] + swap_cores(grad_normed[own_rows:])
        grad_inputs = (
            upstream.astype(jnp.float32)
            + norm_scale * grad_normed
            - values * norm_scale**3 * jnp.mean(values * grad_normed, axis=-1, keepdims=True)
        ).astype(jnp.bfloat16)
        if keep_grad is None:
            keep_grad = grad_inputs
        else:
            keep_grad = jnp.where(section_index == active, grad_inputs, keep_grad)
        if step_index < section_count - 1:
            pairs = [(i, i - 1) for i in range(1, section_count)]
            received = lax.ppermute(grad_inputs, "section", pairs)
    first_grad = keep_grad
    chip_grad = lax.psum_scatter(grad_half, "xy", scatter_dimension=0, tiled=True)
    chip_grad = chip_grad.reshape(2, local_rows, 4, half_width)
    mine_grad = pick(chip_grad, core, 0)
    theirs_grad = swap_cores(pick(chip_grad, other, 0))
    attn_grad = jnp.where(
        core == 0,
        jnp.stack([mine_grad, theirs_grad], axis=2),
        jnp.stack([theirs_grad, mine_grad], axis=2),
    ).reshape(local_rows, 4 * attn_width).astype(jnp.float32)

    input_grad = broadcast_from_first(first_grad, "section")
    grad_all = jnp.concatenate([input_grad, swap_cores(input_grad)], axis=0)
    coords_own = coords.reshape(3, own_rows)
    coords_all = jnp.concatenate([coords_own, swap_cores(coords_own)], axis=1)
    augmented = jnp.concatenate(
        [coords_all, jnp.ones((1, 2 * own_rows), jnp.float32)], axis=0
    )
    embed_half = pick(
        embed_both.reshape(chip_count, 2, embed_rows, width + embed_in.shape[1]), core, 1
    ).reshape(chip_count * embed_rows, width + embed_in.shape[1])
    term_out, term_in = embed_terms(
        embed_half[:, width:], embed_half[:, :width], augmented, grad_all
    )
    terms = jnp.concatenate([term_out, term_in], axis=1).astype(jnp.bfloat16)
    pieces = lax.all_to_all(
        terms.reshape(chip_count, embed_rows, terms.shape[1]), "xy", 0, 0, tiled=False
    )
    summed = jnp.sum(pieces.astype(jnp.float32), axis=0)
    return (
        attn_grad[None],
        input_grad.reshape(micro_count, row_count, width),
        summed[:, :width],
        summed[:, width:],
    )


def solution(mesh):
    sections, fsdp = mesh.devices.shape
    inner = Mesh(mesh.devices.reshape(sections, fsdp // 2, 2), ("section", "xy", "core"))
    placed = (
        P("section", None, FSDP, None),
        P("section", FSDP, None),
        P(None, FSDP, None),
        P(None, FSDP, None),
        P(None, None, FSDP),
        P(("section",) + FSDP, None),
        P(("section",) + FSDP, None),
    )
    outer_specs = (
        P("section", "fsdp", None),
        P(None, "fsdp", None),
        P(("section", "fsdp"), None),
        P(("section", "fsdp"), None),
    )
    mapped = jax.shard_map(
        on_device,
        mesh=inner,
        in_specs=placed,
        out_specs=(
            P("section", FSDP, None),
            P(None, FSDP, None),
            P(("section",) + FSDP, None),
            P(("section",) + FSDP, None),
        ),
        check_vma=False,
    )

    def run(*args):
        outs = mapped(*args)
        return tuple(
            lax.with_sharding_constraint(o, NamedSharding(mesh, s))
            for o, s in zip(outs, outer_specs)
        )

    return run
```

```python
import jax
import jax.numpy as jnp
from jax import lax
from jax.sharding import Mesh, NamedSharding, PartitionSpec as P

HEAD_DIM = 64


EPS = 1e-05

FSDP = ("xy", "core")


def gelu_value(pre):
    return 0.5 * pre * (1.0 + jax.scipy.special.erf(pre / jnp.sqrt(2.0)))


def gelu_slope(pre):
    return 0.5 * (1.0 + jax.scipy.special.erf(pre / jnp.sqrt(2.0))) + pre * jnp.exp(
        -0.5 * pre * pre
    ) / jnp.sqrt(2.0 * jnp.pi)


def normalize(inputs):
    values = inputs.astype(jnp.float32)
    norm_scale = lax.rsqrt(jnp.mean(values * values, axis=-1, keepdims=True) + EPS)
    normed = (values * norm_scale).astype(jnp.bfloat16)
    return (norm_scale, normed)


def swap_cores(value):
    return lax.ppermute(value, "core", [(0, 1), (1, 0)])


def pick(value, index, axis):
    return lax.dynamic_index_in_dim(value, index, axis, keepdims=False)


def heads_major(rows, blocks, heads):
    return rows.reshape(blocks, rows.shape[0] // blocks, heads, HEAD_DIM).transpose(0, 2, 1, 3)


def rows_major(value):
    blocks, heads, block_rows, _ = value.shape
    return value.transpose(0, 2, 1, 3).reshape(blocks * block_rows, heads * HEAD_DIM)


def attention_forward(normed, weights_qkv, segment, blocks):
    width = weights_qkv.shape[1] // 3
    heads = width // HEAD_DIM
    scaling = HEAD_DIM ** (-0.5)
    projected = jnp.dot(
        normed, weights_qkv, preferred_element_type=jnp.float32
    ).astype(jnp.bfloat16)
    queries = heads_major(projected[:, :width], blocks, heads)
    key_rows = heads_major(projected[:, width : 2 * width], blocks, heads)
    value_rows = heads_major(projected[:, 2 * width :], blocks, heads)
    scores = (
        jnp.einsum("bhqd,bhkd->bhqk", queries, key_rows, preferred_element_type=jnp.float32)
        * scaling
    )
    same_session = segment[:, :, None] == segment[:, None, :]
    scores = jnp.where(same_session[:, None], scores, -1e30)
    row_peak = jnp.max(scores, axis=-1, keepdims=True)
    exponent = jnp.exp(scores - row_peak)
    probabilities = exponent / jnp.sum(exponent, axis=-1, keepdims=True)
    prob_rounded = probabilities.astype(jnp.bfloat16)
    attended = rows_major(
        jnp.einsum(
            "bhqk,bhkd->bhqd", prob_rounded, value_rows, preferred_element_type=jnp.float32
        ).astype(jnp.bfloat16)
    )
    return queries, key_rows, value_rows, probabilities, prob_rounded, attended


def attention_backward(forward, upstream, weights_qkv, weights_out):
    queries, key_rows, value_rows, probabilities, prob_rounded, _ = forward
    blocks, heads = queries.shape[:2]
    scaling = HEAD_DIM ** (-0.5)
    grad_attended = jnp.dot(
        upstream, weights_out, preferred_element_type=jnp.float32
    ).astype(jnp.bfloat16)
    grad_heads = heads_major(grad_attended, blocks, heads)
    grad_prob = jnp.einsum(
        "bhqd,bhkd->bhqk", grad_heads, value_rows, preferred_element_type=jnp.float32
    )
    delta = jnp.sum(probabilities * grad_prob, axis=-1, keepdims=True)
    grad_score = lax.optimization_barrier(
        (probabilities * (grad_prob - delta) * scaling).astype(jnp.bfloat16)
    )
    grad_query = jnp.einsum(
        "bhqk,bhkd->bhqd", grad_score, key_rows, preferred_element_type=jnp.float32
    )
    grad_key = jnp.einsum(
        "bhqk,bhqd->bhkd", grad_score, queries, preferred_element_type=jnp.float32
    )
    grad_value = jnp.einsum(
        "bhqk,bhqd->bhkd", prob_rounded, grad_heads, preferred_element_type=jnp.float32
    )
    grad_qkv = jnp.concatenate(
        [
            rows_major(grad_query.astype(jnp.bfloat16)),
            rows_major(grad_key.astype(jnp.bfloat16)),
            rows_major(grad_value.astype(jnp.bfloat16)),
        ],
        axis=1,
    )
    grad_normed = lax.dot_general(
        grad_qkv,
        weights_qkv,
        (((1,), (1,)), ((), ())),
        preferred_element_type=jnp.float32,
    )
    return grad_qkv, grad_normed


def embed_terms(embed_in_q, embed_out_q, aug_rows, grad_rows):
    pre = jnp.dot(embed_in_q.astype(jnp.float32), aug_rows, precision=lax.Precision.HIGHEST)
    hidden = gelu_value(pre).astype(jnp.bfloat16)
    term_out = jnp.dot(hidden, grad_rows, preferred_element_type=jnp.float32)
    grad_hidden = lax.dot_general(
        embed_out_q, grad_rows, (((1,), (1,)), ((), ())), preferred_element_type=jnp.float32
    )
    grad_pre = grad_hidden * gelu_slope(pre)
    term_in = lax.dot_general(
        grad_pre, aug_rows, (((1,), (1,)), ((), ())), precision=lax.Precision.HIGHEST
    )
    return (term_out, term_in)


def broadcast_from_first(block, axis):
    count = lax.axis_size(axis)
    index = lax.axis_index(axis)
    if count == 1:
        return block
    result = jnp.where(index == 0, block, lax.ppermute(block, axis, [(0, 1)]))
    if count > 2:
        back = lax.ppermute(block, axis, [(0, count - 1)])
        result = jnp.where(index == count - 1, back, result)
    if count <= 3:
        return result
    assert count == 4
    half = block.shape[0] // 2
    low = lax.ppermute(result[:half], axis, [(1, 2)])
    high = lax.ppermute(result[half:], axis, [(3, 2)])
    return jnp.where(index == 2, jnp.concatenate([low, high], axis=0), result)


def on_device(saved_inputs, attn_weights, grad_out, segments, coords, embed_in, embed_out):
    section_count = lax.axis_size("section")
    section_index = lax.axis_index("section")
    chip_count = lax.axis_size("xy")
    core = lax.axis_index("core")
    other = 1 - core
    micro_count = saved_inputs.shape[1]
    row_count = saved_inputs.shape[2]
    width = saved_inputs.shape[3]
    local_rows = attn_weights.shape[1]
    attn_width = attn_weights.shape[2] // 4
    half_width = attn_width // 2
    own_rows = micro_count * row_count
    embed_rows = embed_out.shape[0]

    mine = attn_weights[0].reshape(local_rows, 4, 2, half_width)
    given = swap_cores(pick(mine, other, 2))
    kept = pick(mine, core, 2)
    chip_rows = jnp.where(
        core == 0,
        jnp.concatenate([kept, given], axis=0),
        jnp.concatenate([given, kept], axis=0),
    ).reshape(2 * local_rows, 4 * half_width)
    layer = lax.all_gather(chip_rows, "xy", axis=0, tiled=True)
    weights_qkv = layer[:, : 3 * half_width]
    weights_out = layer[:, 3 * half_width :]

    embed_both = lax.all_gather(
        jnp.concatenate([embed_out, embed_in], axis=1), FSDP, axis=0, tiled=True
    )

    inputs_own = saved_inputs[0].reshape(own_rows, width)
    inputs_all = jnp.concatenate([inputs_own, swap_cores(inputs_own)], axis=0)
    segment_own = segments[:, 0, :]
    segment_all = jnp.concatenate([segment_own, swap_cores(segment_own)], axis=0)
    norm_scale_all, normed_all = normalize(inputs_all)
    norm_scale = norm_scale_all[:own_rows]
    values = inputs_own.astype(jnp.float32)
    forward = attention_forward(normed_all, weights_qkv, segment_all, 2 * micro_count)
    attended_all = forward[-1]

    top_grad = grad_out.reshape(own_rows, width)
    received = top_grad
    keep = None
    for step_index in range(section_count):
        active = section_count - 1 - step_index
        upstream = top_grad if step_index == 0 else received
        upstream_all = jnp.concatenate([upstream, swap_cores(upstream)], axis=0)
        grad_qkv, grad_normed = attention_backward(
            forward, upstream_all, weights_qkv, weights_out
        )
        grad_normed = grad_normed[:own_rows] + swap_cores(grad_normed[own_rows:])
        grad_inputs = (
            upstream.astype(jnp.float32)
            + norm_scale * grad_normed
            - values * norm_scale**3 * jnp.mean(values * grad_normed, axis=-1, keepdims=True)
        ).astype(jnp.bfloat16)
        fresh = (grad_qkv, upstream_all, grad_inputs)
        if keep is None:
            keep = fresh
        else:
            valid = section_index == active
            keep = tuple(jnp.where(valid, f, k) for f, k in zip(fresh, keep))
        if step_index < section_count - 1:
            pairs = [(i, i - 1) for i in range(1, section_count)]
            received = lax.ppermute(grad_inputs, "section", pairs)
    qkv_all, up_all, first_grad = keep
    chip_tokens = qkv_all.shape[0]
    left = lax.optimization_barrier(jnp.concatenate([normed_all, up_all], axis=0).T)
    right = jnp.concatenate(
        [
            jnp.concatenate(
                [qkv_all, jnp.zeros((chip_tokens, half_width), qkv_all.dtype)], axis=1
            ),
            jnp.concatenate(
                [jnp.zeros((chip_tokens, 3 * half_width), qkv_all.dtype), attended_all], axis=1
            ),
        ],
        axis=0,
    )
    grad_half = jnp.dot(left, right, preferred_element_type=jnp.float32).astype(jnp.bfloat16)
    chip_grad = lax.psum_scatter(grad_half, "xy", scatter_dimension=0, tiled=True)
    chip_grad = chip_grad.reshape(2, local_rows, 4, half_width)
    mine_grad = pick(chip_grad, core, 0)
    theirs_grad = swap_cores(pick(chip_grad, other, 0))
    attn_grad = jnp.where(
        core == 0,
        jnp.stack([mine_grad, theirs_grad], axis=2),
        jnp.stack([theirs_grad, mine_grad], axis=2),
    ).reshape(local_rows, 4 * attn_width).astype(jnp.float32)

    input_grad = broadcast_from_first(first_grad, "section")
    grad_all = jnp.concatenate([input_grad, swap_cores(input_grad)], axis=0)
    coords_own = coords.reshape(3, own_rows)
    coords_all = jnp.concatenate([coords_own, swap_cores(coords_own)], axis=1)
    augmented = jnp.concatenate(
        [coords_all, jnp.ones((1, 2 * own_rows), jnp.float32)], axis=0
    )
    embed_half = pick(
        embed_both.reshape(chip_count, 2, embed_rows, width + embed_in.shape[1]), core, 1
    ).reshape(chip_count * embed_rows, width + embed_in.shape[1])
    term_out, term_in = embed_terms(
        embed_half[:, width:], embed_half[:, :width], augmented, grad_all
    )
    terms = jnp.concatenate([term_out, term_in], axis=1).astype(jnp.bfloat16)
    pieces = lax.all_to_all(
        terms.reshape(chip_count, embed_rows, terms.shape[1]), "xy", 0, 0, tiled=False
    )
    summed = jnp.sum(pieces.astype(jnp.float32), axis=0)
    return (
        attn_grad[None],
        input_grad.reshape(micro_count, row_count, width),
        summed[:, :width],
        summed[:, width:],
    )


def solution(mesh):
    sections, fsdp = mesh.devices.shape
    inner = Mesh(mesh.devices.reshape(sections, fsdp // 2, 2), ("section", "xy", "core"))
    placed = (
        P("section", None, FSDP, None),
        P("section", FSDP, None),
        P(None, FSDP, None),
        P(None, FSDP, None),
        P(None, None, FSDP),
        P(("section",) + FSDP, None),
        P(("section",) + FSDP, None),
    )
    outer_specs = (
        P("section", "fsdp", None),
        P(None, "fsdp", None),
        P(("section", "fsdp"), None),
        P(("section", "fsdp"), None),
    )
    mapped = jax.shard_map(
        on_device,
        mesh=inner,
        in_specs=placed,
        out_specs=(
            P("section", FSDP, None),
            P(None, FSDP, None),
            P(("section",) + FSDP, None),
            P(("section",) + FSDP, None),
        ),
        check_vma=False,
    )

    def run(*args):
        outs = mapped(*args)
        return tuple(
            lax.with_sharding_constraint(o, NamedSharding(mesh, s))
            for o, s in zip(outs, outer_specs)
        )

    return run
```

```python
import jax
import jax.numpy as jnp
from jax import lax
from jax.sharding import Mesh, NamedSharding, PartitionSpec as P

HEAD_DIM = 64


EPS = 1e-05

FSDP = ("xy", "core")


def gelu_value(pre):
    return 0.5 * pre * (1.0 + jax.scipy.special.erf(pre / jnp.sqrt(2.0)))


def gelu_slope(pre):
    return 0.5 * (1.0 + jax.scipy.special.erf(pre / jnp.sqrt(2.0))) + pre * jnp.exp(
        -0.5 * pre * pre
    ) / jnp.sqrt(2.0 * jnp.pi)


def normalize(inputs):
    values = inputs.astype(jnp.float32)
    norm_scale = lax.rsqrt(jnp.mean(values * values, axis=-1, keepdims=True) + EPS)
    normed = (values * norm_scale).astype(jnp.bfloat16)
    return (norm_scale, normed)


def swap_cores(value):
    return lax.ppermute(value, "core", [(0, 1), (1, 0)])


def pick(value, index, axis):
    return lax.dynamic_index_in_dim(value, index, axis, keepdims=False)


def heads_major(rows, blocks, heads):
    return rows.reshape(blocks, rows.shape[0] // blocks, heads, HEAD_DIM).transpose(0, 2, 1, 3)


def rows_major(value):
    blocks, heads, block_rows, _ = value.shape
    return value.transpose(0, 2, 1, 3).reshape(blocks * block_rows, heads * HEAD_DIM)


def attention_forward(normed, weights_qkv, segment, blocks):
    width = weights_qkv.shape[1] // 3
    heads = width // HEAD_DIM
    scaling = HEAD_DIM ** (-0.5)
    projected = jnp.dot(
        normed, weights_qkv, preferred_element_type=jnp.float32
    ).astype(jnp.bfloat16)
    queries = heads_major(projected[:, :width], blocks, heads)
    key_rows = heads_major(projected[:, width : 2 * width], blocks, heads)
    value_rows = heads_major(projected[:, 2 * width :], blocks, heads)
    scores = (
        jnp.einsum("bhqd,bhkd->bhqk", queries, key_rows, preferred_element_type=jnp.float32)
        * scaling
    )
    same_session = segment[:, :, None] == segment[:, None, :]
    scores = jnp.where(same_session[:, None], scores, -1e30)
    row_peak = jnp.max(scores, axis=-1, keepdims=True)
    exponent = jnp.exp(scores - row_peak)
    probabilities = exponent / jnp.sum(exponent, axis=-1, keepdims=True)
    prob_rounded = probabilities.astype(jnp.bfloat16)
    attended = rows_major(
        jnp.einsum(
            "bhqk,bhkd->bhqd", prob_rounded, value_rows, preferred_element_type=jnp.float32
        ).astype(jnp.bfloat16)
    )
    return queries, key_rows, value_rows, probabilities, prob_rounded, attended


def attention_backward(forward, upstream, weights_qkv, weights_out):
    queries, key_rows, value_rows, probabilities, prob_rounded, _ = forward
    blocks, heads = queries.shape[:2]
    scaling = HEAD_DIM ** (-0.5)
    grad_attended = jnp.dot(
        upstream, weights_out, preferred_element_type=jnp.float32
    ).astype(jnp.bfloat16)
    grad_heads = heads_major(grad_attended, blocks, heads)
    grad_prob = jnp.einsum(
        "bhqd,bhkd->bhqk", grad_heads, value_rows, preferred_element_type=jnp.float32
    )
    delta = jnp.sum(probabilities * grad_prob, axis=-1, keepdims=True)
    grad_score = lax.optimization_barrier(
        (probabilities * (grad_prob - delta) * scaling).astype(jnp.bfloat16)
    )
    grad_query = jnp.einsum(
        "bhqk,bhkd->bhqd", grad_score, key_rows, preferred_element_type=jnp.float32
    )
    grad_key = jnp.einsum(
        "bhqk,bhqd->bhkd", grad_score, queries, preferred_element_type=jnp.float32
    )
    grad_value = jnp.einsum(
        "bhqk,bhqd->bhkd", prob_rounded, grad_heads, preferred_element_type=jnp.float32
    )
    stacked = jnp.stack([grad_query, grad_key, grad_value]).astype(jnp.bfloat16)
    block_rows = stacked.shape[3]
    grad_qkv = stacked.transpose(1, 3, 0, 2, 4).reshape(
        blocks * block_rows, 3 * heads * HEAD_DIM
    )
    grad_normed = lax.dot_general(
        grad_qkv,
        weights_qkv,
        (((1,), (1,)), ((), ())),
        preferred_element_type=jnp.float32,
    )
    return grad_qkv, grad_normed


def embed_terms(embed_in_q, embed_out_q, aug_rows, grad_rows):
    pre = jnp.dot(embed_in_q.astype(jnp.float32), aug_rows, precision=lax.Precision.HIGHEST)
    hidden = gelu_value(pre).astype(jnp.bfloat16)
    term_out = jnp.dot(hidden, grad_rows, preferred_element_type=jnp.float32)
    grad_hidden = lax.dot_general(
        embed_out_q, grad_rows, (((1,), (1,)), ((), ())), preferred_element_type=jnp.float32
    )
    grad_pre = grad_hidden * gelu_slope(pre)
    term_in = lax.dot_general(
        grad_pre, aug_rows, (((1,), (1,)), ((), ())), precision=lax.Precision.HIGHEST
    )
    return (term_out, term_in)


def broadcast_from_first(block, axis):
    count = lax.axis_size(axis)
    index = lax.axis_index(axis)
    if count == 1:
        return block
    result = jnp.where(index == 0, block, lax.ppermute(block, axis, [(0, 1)]))
    if count > 2:
        back = lax.ppermute(block, axis, [(0, count - 1)])
        result = jnp.where(index == count - 1, back, result)
    if count <= 3:
        return result
    assert count == 4
    half = block.shape[0] // 2
    low = lax.ppermute(result[:half], axis, [(1, 2)])
    high = lax.ppermute(result[half:], axis, [(3, 2)])
    return jnp.where(index == 2, jnp.concatenate([low, high], axis=0), result)


def on_device(saved_inputs, attn_weights, grad_out, segments, coords, embed_in, embed_out):
    section_count = lax.axis_size("section")
    section_index = lax.axis_index("section")
    chip_count = lax.axis_size("xy")
    core = lax.axis_index("core")
    other = 1 - core
    micro_count = saved_inputs.shape[1]
    row_count = saved_inputs.shape[2]
    width = saved_inputs.shape[3]
    local_rows = attn_weights.shape[1]
    attn_width = attn_weights.shape[2] // 4
    half_width = attn_width // 2
    own_rows = micro_count * row_count
    embed_rows = embed_out.shape[0]

    mine = attn_weights[0].reshape(local_rows, 4, 2, half_width)
    given = swap_cores(pick(mine, other, 2))
    kept = pick(mine, core, 2)
    chip_rows = jnp.where(
        core == 0,
        jnp.concatenate([kept, given], axis=0),
        jnp.concatenate([given, kept], axis=0),
    ).reshape(2 * local_rows, 4 * half_width)
    layer = lax.all_gather(chip_rows, "xy", axis=0, tiled=True)
    weights_qkv = layer[:, : 3 * half_width]
    weights_out = layer[:, 3 * half_width :]

    embed_both = lax.all_gather(
        jnp.concatenate([embed_out, embed_in], axis=1), FSDP, axis=0, tiled=True
    )

    inputs_own = saved_inputs[0].reshape(own_rows, width)
    inputs_all = jnp.concatenate([inputs_own, swap_cores(inputs_own)], axis=0)
    segment_own = segments[:, 0, :]
    segment_all = jnp.concatenate([segment_own, swap_cores(segment_own)], axis=0)
    norm_scale_all, normed_all = normalize(inputs_all)
    norm_scale = norm_scale_all[:own_rows]
    values = inputs_own.astype(jnp.float32)
    forward = attention_forward(normed_all, weights_qkv, segment_all, 2 * micro_count)
    attended_all = forward[-1]

    top_grad = grad_out.reshape(own_rows, width)
    received = top_grad
    keep = None
    for step_index in range(section_count):
        active = section_count - 1 - step_index
        upstream = top_grad if step_index == 0 else received
        upstream_all = jnp.concatenate([upstream, swap_cores(upstream)], axis=0)
        grad_qkv, grad_normed = attention_backward(
            forward, upstream_all, weights_qkv, weights_out
        )
        grad_normed = grad_normed[:own_rows] + swap_cores(grad_normed[own_rows:])
        grad_inputs = (
            upstream.astype(jnp.float32)
            + norm_scale * grad_normed
            - values * norm_scale**3 * jnp.mean(values * grad_normed, axis=-1, keepdims=True)
        ).astype(jnp.bfloat16)
        fresh = (grad_qkv, upstream_all, grad_inputs)
        if keep is None:
            keep = fresh
        else:
            valid = section_index == active
            keep = tuple(jnp.where(valid, f, k) for f, k in zip(fresh, keep))
        if step_index < section_count - 1:
            pairs = [(i, i - 1) for i in range(1, section_count)]
            received = lax.ppermute(grad_inputs, "section", pairs)
    qkv_all, up_all, first_grad = keep
    chip_tokens = qkv_all.shape[0]
    left = lax.optimization_barrier(jnp.concatenate([normed_all, up_all], axis=0).T)
    right = jnp.concatenate(
        [
            jnp.concatenate(
                [qkv_all, jnp.zeros((chip_tokens, half_width), qkv_all.dtype)], axis=1
            ),
            jnp.concatenate(
                [jnp.zeros((chip_tokens, 3 * half_width), qkv_all.dtype), attended_all], axis=1
            ),
        ],
        axis=0,
    )
    grad_half = jnp.dot(left, right, preferred_element_type=jnp.float32).astype(jnp.bfloat16)
    chip_grad = lax.psum_scatter(grad_half, "xy", scatter_dimension=0, tiled=True)
    chip_grad = chip_grad.reshape(2, local_rows, 4, half_width)
    mine_grad = pick(chip_grad, core, 0)
    theirs_grad = swap_cores(pick(chip_grad, other, 0))
    attn_grad = jnp.where(
        core == 0,
        jnp.stack([mine_grad, theirs_grad], axis=2),
        jnp.stack([theirs_grad, mine_grad], axis=2),
    ).reshape(local_rows, 4 * attn_width).astype(jnp.float32)

    input_grad = broadcast_from_first(first_grad, "section")
    grad_all = jnp.concatenate([input_grad, swap_cores(input_grad)], axis=0)
    coords_own = coords.reshape(3, own_rows)
    coords_all = jnp.concatenate([coords_own, swap_cores(coords_own)], axis=1)
    augmented = jnp.concatenate(
        [coords_all, jnp.ones((1, 2 * own_rows), jnp.float32)], axis=0
    )
    embed_half = pick(
        embed_both.reshape(chip_count, 2, embed_rows, width + embed_in.shape[1]), core, 1
    ).reshape(chip_count * embed_rows, width + embed_in.shape[1])
    term_out, term_in = embed_terms(
        embed_half[:, width:], embed_half[:, :width], augmented, grad_all
    )
    terms = jnp.concatenate([term_out, term_in], axis=1).astype(jnp.bfloat16)
    pieces = lax.all_to_all(
        terms.reshape(chip_count, embed_rows, terms.shape[1]), "xy", 0, 0, tiled=False
    )
    summed = jnp.sum(pieces.astype(jnp.float32), axis=0)
    return (
        attn_grad[None],
        input_grad.reshape(micro_count, row_count, width),
        summed[:, :width],
        summed[:, width:],
    )


def solution(mesh):
    sections, fsdp = mesh.devices.shape
    inner = Mesh(mesh.devices.reshape(sections, fsdp // 2, 2), ("section", "xy", "core"))
    placed = (
        P("section", None, FSDP, None),
        P("section", FSDP, None),
        P(None, FSDP, None),
        P(None, FSDP, None),
        P(None, None, FSDP),
        P(("section",) + FSDP, None),
        P(("section",) + FSDP, None),
    )
    outer_specs = (
        P("section", "fsdp", None),
        P(None, "fsdp", None),
        P(("section", "fsdp"), None),
        P(("section", "fsdp"), None),
    )
    mapped = jax.shard_map(
        on_device,
        mesh=inner,
        in_specs=placed,
        out_specs=(
            P("section", FSDP, None),
            P(None, FSDP, None),
            P(("section",) + FSDP, None),
            P(("section",) + FSDP, None),
        ),
        check_vma=False,
    )

    def run(*args):
        outs = mapped(*args)
        return tuple(
            lax.with_sharding_constraint(o, NamedSharding(mesh, s))
            for o, s in zip(outs, outer_specs)
        )

    return run
```

```python
import jax
import jax.numpy as jnp
from jax import lax
from jax.sharding import Mesh, NamedSharding, PartitionSpec as P

HEAD_DIM = 64


EPS = 1e-05

FSDP = ("xy", "core")


def gelu_value(pre):
    return 0.5 * pre * (1.0 + jax.scipy.special.erf(pre / jnp.sqrt(2.0)))


def gelu_slope(pre):
    return 0.5 * (1.0 + jax.scipy.special.erf(pre / jnp.sqrt(2.0))) + pre * jnp.exp(
        -0.5 * pre * pre
    ) / jnp.sqrt(2.0 * jnp.pi)


def normalize(inputs):
    values = inputs.astype(jnp.float32)
    norm_scale = lax.rsqrt(jnp.mean(values * values, axis=-1, keepdims=True) + EPS)
    normed = (values * norm_scale).astype(jnp.bfloat16)
    return (norm_scale, normed)


def swap_cores(value):
    return lax.ppermute(value, "core", [(0, 1), (1, 0)])


def pick(value, index, axis):
    return lax.dynamic_index_in_dim(value, index, axis, keepdims=False)


def heads_major(rows, blocks, heads):
    return rows.reshape(blocks, rows.shape[0] // blocks, heads, HEAD_DIM).transpose(0, 2, 1, 3)


def rows_major(value):
    blocks, heads, block_rows, _ = value.shape
    return value.transpose(0, 2, 1, 3).reshape(blocks * block_rows, heads * HEAD_DIM)


def attention_forward(normed, weights_qkv, segment, blocks):
    width = weights_qkv.shape[1] // 3
    heads = width // HEAD_DIM
    scaling = HEAD_DIM ** (-0.5)
    projected = jnp.dot(
        normed, weights_qkv, preferred_element_type=jnp.float32
    ).astype(jnp.bfloat16)
    queries = heads_major(projected[:, :width], blocks, heads)
    key_rows = heads_major(projected[:, width : 2 * width], blocks, heads)
    value_rows = heads_major(projected[:, 2 * width :], blocks, heads)
    scores = (
        jnp.einsum("bhqd,bhkd->bhqk", queries, key_rows, preferred_element_type=jnp.float32)
        * scaling
    )
    same_session = segment[:, :, None] == segment[:, None, :]
    scores = jnp.where(same_session[:, None], scores, -1e30)
    row_peak = jnp.max(scores, axis=-1, keepdims=True)
    exponent = jnp.exp(scores - row_peak)
    probabilities = exponent / jnp.sum(exponent, axis=-1, keepdims=True)
    prob_rounded = probabilities.astype(jnp.bfloat16)
    attended = rows_major(
        jnp.einsum(
            "bhqk,bhkd->bhqd", prob_rounded, value_rows, preferred_element_type=jnp.float32
        ).astype(jnp.bfloat16)
    )
    return queries, key_rows, value_rows, probabilities, prob_rounded, attended


def attention_backward(forward, upstream, weights_qkv, weights_out):
    queries, key_rows, value_rows, probabilities, prob_rounded, _ = forward
    blocks, heads = queries.shape[:2]
    scaling = HEAD_DIM ** (-0.5)
    grad_heads = jnp.einsum(
        "bqd,dhe->bhqe",
        upstream.reshape(blocks, upstream.shape[0] // blocks, upstream.shape[1]),
        weights_out.reshape(weights_out.shape[0], heads, HEAD_DIM),
        preferred_element_type=jnp.float32,
    ).astype(jnp.bfloat16)
    grad_prob = jnp.einsum(
        "bhqd,bhkd->bhqk", grad_heads, value_rows, preferred_element_type=jnp.float32
    )
    delta = jnp.sum(probabilities * grad_prob, axis=-1, keepdims=True)
    grad_score = lax.optimization_barrier(
        (probabilities * (grad_prob - delta) * scaling).astype(jnp.bfloat16)
    )
    grad_query = jnp.einsum(
        "bhqk,bhkd->bhqd", grad_score, key_rows, preferred_element_type=jnp.float32
    )
    grad_key = jnp.einsum(
        "bhqk,bhqd->bhkd", grad_score, queries, preferred_element_type=jnp.float32
    )
    grad_value = jnp.einsum(
        "bhqk,bhqd->bhkd", prob_rounded, grad_heads, preferred_element_type=jnp.float32
    )
    stacked = jnp.stack([grad_query, grad_key, grad_value]).astype(jnp.bfloat16)
    block_rows = stacked.shape[3]
    grad_qkv = stacked.transpose(1, 3, 0, 2, 4).reshape(
        blocks * block_rows, 3 * heads * HEAD_DIM
    )
    grad_normed = lax.dot_general(
        grad_qkv,
        weights_qkv,
        (((1,), (1,)), ((), ())),
        preferred_element_type=jnp.float32,
    )
    return grad_qkv, grad_normed


def embed_terms(embed_in_q, embed_out_q, aug_rows, grad_rows):
    pre = jnp.dot(embed_in_q.astype(jnp.float32), aug_rows, precision=lax.Precision.HIGHEST)
    hidden = gelu_value(pre).astype(jnp.bfloat16)
    term_out = jnp.dot(hidden, grad_rows, preferred_element_type=jnp.float32)
    grad_hidden = lax.dot_general(
        embed_out_q, grad_rows, (((1,), (1,)), ((), ())), preferred_element_type=jnp.float32
    )
    grad_pre = grad_hidden * gelu_slope(pre)
    term_in = lax.dot_general(
        grad_pre, aug_rows, (((1,), (1,)), ((), ())), precision=lax.Precision.HIGHEST
    )
    return (term_out, term_in)


def broadcast_from_first(block, axis):
    count = lax.axis_size(axis)
    index = lax.axis_index(axis)
    if count == 1:
        return block
    result = jnp.where(index == 0, block, lax.ppermute(block, axis, [(0, 1)]))
    if count > 2:
        back = lax.ppermute(block, axis, [(0, count - 1)])
        result = jnp.where(index == count - 1, back, result)
    if count <= 3:
        return result
    assert count == 4
    half = block.shape[0] // 2
    low = lax.ppermute(result[:half], axis, [(1, 2)])
    high = lax.ppermute(result[half:], axis, [(3, 2)])
    return jnp.where(index == 2, jnp.concatenate([low, high], axis=0), result)


def on_device(saved_inputs, attn_weights, grad_out, segments, coords, embed_in, embed_out):
    section_count = lax.axis_size("section")
    section_index = lax.axis_index("section")
    chip_count = lax.axis_size("xy")
    core = lax.axis_index("core")
    other = 1 - core
    micro_count = saved_inputs.shape[1]
    row_count = saved_inputs.shape[2]
    width = saved_inputs.shape[3]
    local_rows = attn_weights.shape[1]
    attn_width = attn_weights.shape[2] // 4
    half_width = attn_width // 2
    own_rows = micro_count * row_count
    embed_rows = embed_out.shape[0]

    mine = attn_weights[0].reshape(local_rows, 4, 2, half_width)
    given = swap_cores(pick(mine, other, 2))
    kept = pick(mine, core, 2)
    chip_rows = jnp.where(
        core == 0,
        jnp.concatenate([kept, given], axis=0),
        jnp.concatenate([given, kept], axis=0),
    ).reshape(2 * local_rows, 4 * half_width)
    layer = lax.all_gather(chip_rows, "xy", axis=0, tiled=True)
    weights_qkv = layer[:, : 3 * half_width]
    weights_out = layer[:, 3 * half_width :]

    embed_both = lax.all_gather(
        jnp.concatenate([embed_out, embed_in], axis=1), FSDP, axis=0, tiled=True
    )

    inputs_own = saved_inputs[0].reshape(own_rows, width)
    inputs_all = jnp.concatenate([inputs_own, swap_cores(inputs_own)], axis=0)
    segment_own = segments[:, 0, :]
    segment_all = jnp.concatenate([segment_own, swap_cores(segment_own)], axis=0)
    norm_scale_all, normed_all = normalize(inputs_all)
    norm_scale = norm_scale_all[:own_rows]
    values = inputs_own.astype(jnp.float32)
    forward = attention_forward(normed_all, weights_qkv, segment_all, 2 * micro_count)
    attended_all = forward[-1]

    top_grad = grad_out.reshape(own_rows, width)
    received = top_grad
    keep = None
    for step_index in range(section_count):
        active = section_count - 1 - step_index
        upstream = top_grad if step_index == 0 else received
        upstream_all = jnp.concatenate([upstream, swap_cores(upstream)], axis=0)
        grad_qkv, grad_normed = attention_backward(
            forward, upstream_all, weights_qkv, weights_out
        )
        grad_normed = grad_normed[:own_rows] + swap_cores(grad_normed[own_rows:])
        grad_inputs = (
            upstream.astype(jnp.float32)
            + norm_scale * grad_normed
            - values * norm_scale**3 * jnp.mean(values * grad_normed, axis=-1, keepdims=True)
        ).astype(jnp.bfloat16)
        fresh = (grad_qkv, upstream_all, grad_inputs)
        if keep is None:
            keep = fresh
        else:
            valid = section_index == active
            keep = tuple(jnp.where(valid, f, k) for f, k in zip(fresh, keep))
        if step_index < section_count - 1:
            pairs = [(i, i - 1) for i in range(1, section_count)]
            received = lax.ppermute(grad_inputs, "section", pairs)
    qkv_all, up_all, first_grad = keep
    chip_tokens = qkv_all.shape[0]
    left = lax.optimization_barrier(jnp.concatenate([normed_all, up_all], axis=0).T)
    right = jnp.concatenate(
        [
            jnp.concatenate(
                [qkv_all, jnp.zeros((chip_tokens, half_width), qkv_all.dtype)], axis=1
            ),
            jnp.concatenate(
                [jnp.zeros((chip_tokens, 3 * half_width), qkv_all.dtype), attended_all], axis=1
            ),
        ],
        axis=0,
    )
    grad_half = jnp.dot(left, right, preferred_element_type=jnp.float32).astype(jnp.bfloat16)
    chip_grad = lax.psum_scatter(grad_half, "xy", scatter_dimension=0, tiled=True)
    chip_grad = chip_grad.reshape(2, local_rows, 4, half_width)
    mine_grad = pick(chip_grad, core, 0)
    theirs_grad = swap_cores(pick(chip_grad, other, 0))
    attn_grad = jnp.where(
        core == 0,
        jnp.stack([mine_grad, theirs_grad], axis=2),
        jnp.stack([theirs_grad, mine_grad], axis=2),
    ).reshape(local_rows, 4 * attn_width).astype(jnp.float32)

    input_grad = broadcast_from_first(first_grad, "section")
    grad_all = jnp.concatenate([input_grad, swap_cores(input_grad)], axis=0)
    coords_own = coords.reshape(3, own_rows)
    coords_all = jnp.concatenate([coords_own, swap_cores(coords_own)], axis=1)
    augmented = jnp.concatenate(
        [coords_all, jnp.ones((1, 2 * own_rows), jnp.float32)], axis=0
    )
    embed_half = pick(
        embed_both.reshape(chip_count, 2, embed_rows, width + embed_in.shape[1]), core, 1
    ).reshape(chip_count * embed_rows, width + embed_in.shape[1])
    term_out, term_in = embed_terms(
        embed_half[:, width:], embed_half[:, :width], augmented, grad_all
    )
    terms = jnp.concatenate([term_out, term_in], axis=1).astype(jnp.bfloat16)
    pieces = lax.all_to_all(
        terms.reshape(chip_count, embed_rows, terms.shape[1]), "xy", 0, 0, tiled=False
    )
    summed = jnp.sum(pieces.astype(jnp.float32), axis=0)
    return (
        attn_grad[None],
        input_grad.reshape(micro_count, row_count, width),
        summed[:, :width],
        summed[:, width:],
    )


def solution(mesh):
    sections, fsdp = mesh.devices.shape
    inner = Mesh(mesh.devices.reshape(sections, fsdp // 2, 2), ("section", "xy", "core"))
    placed = (
        P("section", None, FSDP, None),
        P("section", FSDP, None),
        P(None, FSDP, None),
        P(None, FSDP, None),
        P(None, None, FSDP),
        P(("section",) + FSDP, None),
        P(("section",) + FSDP, None),
    )
    outer_specs = (
        P("section", "fsdp", None),
        P(None, "fsdp", None),
        P(("section", "fsdp"), None),
        P(("section", "fsdp"), None),
    )
    mapped = jax.shard_map(
        on_device,
        mesh=inner,
        in_specs=placed,
        out_specs=(
            P("section", FSDP, None),
            P(None, FSDP, None),
            P(("section",) + FSDP, None),
            P(("section",) + FSDP, None),
        ),
        check_vma=False,
    )

    def run(*args):
        outs = mapped(*args)
        return tuple(
            lax.with_sharding_constraint(o, NamedSharding(mesh, s))
            for o, s in zip(outs, outer_specs)
        )

    return run
```

```python
import jax
import jax.numpy as jnp
from jax import lax
from jax.sharding import Mesh, NamedSharding, PartitionSpec as P

HEAD_DIM = 64


EPS = 1e-05

FSDP = ("xy", "core")


def gelu_value(pre):
    return 0.5 * pre * (1.0 + jax.scipy.special.erf(pre / jnp.sqrt(2.0)))


def gelu_slope(pre):
    return 0.5 * (1.0 + jax.scipy.special.erf(pre / jnp.sqrt(2.0))) + pre * jnp.exp(
        -0.5 * pre * pre
    ) / jnp.sqrt(2.0 * jnp.pi)


def normalize(inputs):
    values = inputs.astype(jnp.float32)
    norm_scale = lax.rsqrt(jnp.mean(values * values, axis=-1, keepdims=True) + EPS)
    normed = (values * norm_scale).astype(jnp.bfloat16)
    return (norm_scale, normed)


def swap_cores(value):
    return lax.ppermute(value, "core", [(0, 1), (1, 0)])


def pick(value, index, axis):
    return lax.dynamic_index_in_dim(value, index, axis, keepdims=False)


def heads_major(rows, blocks, heads):
    return rows.reshape(blocks, rows.shape[0] // blocks, heads, HEAD_DIM).transpose(0, 2, 1, 3)


def rows_major(value):
    blocks, heads, block_rows, _ = value.shape
    return value.transpose(0, 2, 1, 3).reshape(blocks * block_rows, heads * HEAD_DIM)


def attention_forward(normed, weights_qkv, segment, blocks):
    width = weights_qkv.shape[1] // 3
    heads = width // HEAD_DIM
    scaling = HEAD_DIM ** (-0.5)
    projected = jnp.dot(
        normed, weights_qkv, preferred_element_type=jnp.float32
    ).astype(jnp.bfloat16)
    queries = heads_major(projected[:, :width], blocks, heads)
    key_rows = heads_major(projected[:, width : 2 * width], blocks, heads)
    value_rows = heads_major(projected[:, 2 * width :], blocks, heads)
    scores = (
        jnp.einsum("bhqd,bhkd->bhqk", queries, key_rows, preferred_element_type=jnp.float32)
        * scaling
    )
    same_session = segment[:, :, None] == segment[:, None, :]
    scores = jnp.where(same_session[:, None], scores, -1e30)
    row_peak = jnp.max(scores, axis=-1, keepdims=True)
    exponent = jnp.exp(scores - row_peak)
    probabilities = exponent / jnp.sum(exponent, axis=-1, keepdims=True)
    prob_rounded = probabilities.astype(jnp.bfloat16)
    attended = rows_major(
        jnp.einsum(
            "bhqk,bhkd->bhqd", prob_rounded, value_rows, preferred_element_type=jnp.float32
        ).astype(jnp.bfloat16)
    )
    return queries, key_rows, value_rows, probabilities, prob_rounded, attended


def attention_backward(forward, upstream, weights_qkv, weights_out):
    queries, key_rows, value_rows, probabilities, prob_rounded, _ = forward
    blocks, heads = queries.shape[:2]
    scaling = HEAD_DIM ** (-0.5)
    grad_heads = jnp.einsum(
        "bqd,dhe->bhqe",
        upstream.reshape(blocks, upstream.shape[0] // blocks, upstream.shape[1]),
        weights_out.reshape(weights_out.shape[0], heads, HEAD_DIM),
        preferred_element_type=jnp.float32,
    ).astype(jnp.bfloat16)
    grad_prob = jnp.einsum(
        "bhqd,bhkd->bhqk", grad_heads, value_rows, preferred_element_type=jnp.float32
    )
    delta = jnp.sum(probabilities * grad_prob, axis=-1, keepdims=True)
    grad_score = lax.optimization_barrier(
        (probabilities * (grad_prob - delta) * scaling).astype(jnp.bfloat16)
    )
    grad_query = jnp.einsum(
        "bhqk,bhkd->bhqd", grad_score, key_rows, preferred_element_type=jnp.float32
    )
    grad_key = jnp.einsum(
        "bhqk,bhqd->bhkd", grad_score, queries, preferred_element_type=jnp.float32
    )
    grad_value = jnp.einsum(
        "bhqk,bhqd->bhkd", prob_rounded, grad_heads, preferred_element_type=jnp.float32
    )
    stacked = jnp.stack([grad_query, grad_key, grad_value]).astype(jnp.bfloat16)
    block_rows = stacked.shape[3]
    grad_normed = jnp.einsum(
        "sbhqe,dshe->bqd",
        stacked,
        weights_qkv.reshape(weights_qkv.shape[0], 3, heads, HEAD_DIM),
        preferred_element_type=jnp.float32,
    ).reshape(blocks * block_rows, weights_qkv.shape[0])
    return stacked, grad_normed


def embed_terms(embed_in_q, embed_out_q, aug_rows, grad_rows):
    pre = jnp.dot(embed_in_q.astype(jnp.float32), aug_rows, precision=lax.Precision.HIGHEST)
    hidden = gelu_value(pre).astype(jnp.bfloat16)
    term_out = jnp.dot(hidden, grad_rows, preferred_element_type=jnp.float32)
    grad_hidden = lax.dot_general(
        embed_out_q, grad_rows, (((1,), (1,)), ((), ())), preferred_element_type=jnp.float32
    )
    grad_pre = grad_hidden * gelu_slope(pre)
    term_in = lax.dot_general(
        grad_pre, aug_rows, (((1,), (1,)), ((), ())), precision=lax.Precision.HIGHEST
    )
    return (term_out, term_in)


def broadcast_from_first(block, axis):
    count = lax.axis_size(axis)
    index = lax.axis_index(axis)
    if count == 1:
        return block
    result = jnp.where(index == 0, block, lax.ppermute(block, axis, [(0, 1)]))
    if count > 2:
        back = lax.ppermute(block, axis, [(0, count - 1)])
        result = jnp.where(index == count - 1, back, result)
    if count <= 3:
        return result
    assert count == 4
    half = block.shape[0] // 2
    low = lax.ppermute(result[:half], axis, [(1, 2)])
    high = lax.ppermute(result[half:], axis, [(3, 2)])
    return jnp.where(index == 2, jnp.concatenate([low, high], axis=0), result)


def on_device(saved_inputs, attn_weights, grad_out, segments, coords, embed_in, embed_out):
    section_count = lax.axis_size("section")
    section_index = lax.axis_index("section")
    chip_count = lax.axis_size("xy")
    core = lax.axis_index("core")
    other = 1 - core
    micro_count = saved_inputs.shape[1]
    row_count = saved_inputs.shape[2]
    width = saved_inputs.shape[3]
    local_rows = attn_weights.shape[1]
    attn_width = attn_weights.shape[2] // 4
    half_width = attn_width // 2
    own_rows = micro_count * row_count
    embed_rows = embed_out.shape[0]

    mine = attn_weights[0].reshape(local_rows, 4, 2, half_width)
    given = swap_cores(pick(mine, other, 2))
    kept = pick(mine, core, 2)
    chip_rows = jnp.where(
        core == 0,
        jnp.concatenate([kept, given], axis=0),
        jnp.concatenate([given, kept], axis=0),
    ).reshape(2 * local_rows, 4 * half_width)
    layer = lax.all_gather(chip_rows, "xy", axis=0, tiled=True)
    weights_qkv = layer[:, : 3 * half_width]
    weights_out = layer[:, 3 * half_width :]

    embed_both = lax.all_gather(
        jnp.concatenate([embed_out, embed_in], axis=1), FSDP, axis=0, tiled=True
    )

    inputs_own = saved_inputs[0].reshape(own_rows, width)
    inputs_all = jnp.concatenate([inputs_own, swap_cores(inputs_own)], axis=0)
    segment_own = segments[:, 0, :]
    segment_all = jnp.concatenate([segment_own, swap_cores(segment_own)], axis=0)
    norm_scale_all, normed_all = normalize(inputs_all)
    norm_scale = norm_scale_all[:own_rows]
    values = inputs_own.astype(jnp.float32)
    forward = attention_forward(normed_all, weights_qkv, segment_all, 2 * micro_count)
    attended_all = forward[-1]

    top_grad = grad_out.reshape(own_rows, width)
    received = top_grad
    keep = None
    for step_index in range(section_count):
        active = section_count - 1 - step_index
        upstream = top_grad if step_index == 0 else received
        upstream_all = jnp.concatenate([upstream, swap_cores(upstream)], axis=0)
        grad_qkv, grad_normed = attention_backward(
            forward, upstream_all, weights_qkv, weights_out
        )
        grad_normed = grad_normed[:own_rows] + swap_cores(grad_normed[own_rows:])
        grad_inputs = (
            upstream.astype(jnp.float32)
            + norm_scale * grad_normed
            - values * norm_scale**3 * jnp.mean(values * grad_normed, axis=-1, keepdims=True)
        ).astype(jnp.bfloat16)
        fresh = (grad_qkv, upstream_all, grad_inputs)
        if keep is None:
            keep = fresh
        else:
            valid = section_index == active
            keep = tuple(jnp.where(valid, f, k) for f, k in zip(fresh, keep))
        if step_index < section_count - 1:
            pairs = [(i, i - 1) for i in range(1, section_count)]
            received = lax.ppermute(grad_inputs, "section", pairs)
    stacked_all, up_all, first_grad = keep
    qkv_all = stacked_all.transpose(1, 3, 0, 2, 4).reshape(
        up_all.shape[0], 3 * half_width
    )
    chip_tokens = qkv_all.shape[0]
    left = lax.optimization_barrier(jnp.concatenate([normed_all, up_all], axis=0).T)
    right = jnp.concatenate(
        [
            jnp.concatenate(
                [qkv_all, jnp.zeros((chip_tokens, half_width), qkv_all.dtype)], axis=1
            ),
            jnp.concatenate(
                [jnp.zeros((chip_tokens, 3 * half_width), qkv_all.dtype), attended_all], axis=1
            ),
        ],
        axis=0,
    )
    grad_half = jnp.dot(left, right, preferred_element_type=jnp.float32).astype(jnp.bfloat16)
    chip_grad = lax.psum_scatter(grad_half, "xy", scatter_dimension=0, tiled=True)
    chip_grad = chip_grad.reshape(2, local_rows, 4, half_width)
    mine_grad = pick(chip_grad, core, 0)
    theirs_grad = swap_cores(pick(chip_grad, other, 0))
    attn_grad = jnp.where(
        core == 0,
        jnp.stack([mine_grad, theirs_grad], axis=2),
        jnp.stack([theirs_grad, mine_grad], axis=2),
    ).reshape(local_rows, 4 * attn_width).astype(jnp.float32)

    input_grad = broadcast_from_first(first_grad, "section")
    grad_all = jnp.concatenate([input_grad, swap_cores(input_grad)], axis=0)
    coords_own = coords.reshape(3, own_rows)
    coords_all = jnp.concatenate([coords_own, swap_cores(coords_own)], axis=1)
    augmented = jnp.concatenate(
        [coords_all, jnp.ones((1, 2 * own_rows), jnp.float32)], axis=0
    )
    embed_half = pick(
        embed_both.reshape(chip_count, 2, embed_rows, width + embed_in.shape[1]), core, 1
    ).reshape(chip_count * embed_rows, width + embed_in.shape[1])
    term_out, term_in = embed_terms(
        embed_half[:, width:], embed_half[:, :width], augmented, grad_all
    )
    terms = jnp.concatenate([term_out, term_in], axis=1).astype(jnp.bfloat16)
    pieces = lax.all_to_all(
        terms.reshape(chip_count, embed_rows, terms.shape[1]), "xy", 0, 0, tiled=False
    )
    summed = jnp.sum(pieces.astype(jnp.float32), axis=0)
    return (
        attn_grad[None],
        input_grad.reshape(micro_count, row_count, width),
        summed[:, :width],
        summed[:, width:],
    )


def solution(mesh):
    sections, fsdp = mesh.devices.shape
    inner = Mesh(mesh.devices.reshape(sections, fsdp // 2, 2), ("section", "xy", "core"))
    placed = (
        P("section", None, FSDP, None),
        P("section", FSDP, None),
        P(None, FSDP, None),
        P(None, FSDP, None),
        P(None, None, FSDP),
        P(("section",) + FSDP, None),
        P(("section",) + FSDP, None),
    )
    outer_specs = (
        P("section", "fsdp", None),
        P(None, "fsdp", None),
        P(("section", "fsdp"), None),
        P(("section", "fsdp"), None),
    )
    mapped = jax.shard_map(
        on_device,
        mesh=inner,
        in_specs=placed,
        out_specs=(
            P("section", FSDP, None),
            P(None, FSDP, None),
            P(("section",) + FSDP, None),
            P(("section",) + FSDP, None),
        ),
        check_vma=False,
    )

    def run(*args):
        outs = mapped(*args)
        return tuple(
            lax.with_sharding_constraint(o, NamedSharding(mesh, s))
            for o, s in zip(outs, outer_specs)
        )

    return run
```

```python
import jax
import jax.numpy as jnp
from jax import lax
from jax.sharding import Mesh, NamedSharding, PartitionSpec as P

HEAD_DIM = 64


EPS = 1e-05

FSDP = ("xy", "core")


def gelu_value(pre):
    return 0.5 * pre * (1.0 + jax.scipy.special.erf(pre / jnp.sqrt(2.0)))


def gelu_slope(pre):
    return 0.5 * (1.0 + jax.scipy.special.erf(pre / jnp.sqrt(2.0))) + pre * jnp.exp(
        -0.5 * pre * pre
    ) / jnp.sqrt(2.0 * jnp.pi)


def normalize(inputs):
    values = inputs.astype(jnp.float32)
    norm_scale = lax.rsqrt(jnp.mean(values * values, axis=-1, keepdims=True) + EPS)
    normed = (values * norm_scale).astype(jnp.bfloat16)
    return (norm_scale, normed)


def swap_cores(value):
    return lax.ppermute(value, "core", [(0, 1), (1, 0)])


def pick(value, index, axis):
    return lax.dynamic_index_in_dim(value, index, axis, keepdims=False)


def heads_major(rows, blocks, heads):
    return rows.reshape(blocks, rows.shape[0] // blocks, heads, HEAD_DIM).transpose(0, 2, 1, 3)


def rows_major(value):
    blocks, heads, block_rows, _ = value.shape
    return value.transpose(0, 2, 1, 3).reshape(blocks * block_rows, heads * HEAD_DIM)


def attention_forward(normed, weights_qkv, segment, blocks):
    width = weights_qkv.shape[1] // 3
    heads = width // HEAD_DIM
    scaling = HEAD_DIM ** (-0.5)
    projected = jnp.dot(
        normed, weights_qkv, preferred_element_type=jnp.float32
    ).astype(jnp.bfloat16)
    split_heads = projected.reshape(
        blocks, projected.shape[0] // blocks, 3, heads, HEAD_DIM
    ).transpose(2, 0, 3, 1, 4)
    queries, key_rows, value_rows = split_heads[0], split_heads[1], split_heads[2]
    scores = (
        jnp.einsum("bhqd,bhkd->bhqk", queries, key_rows, preferred_element_type=jnp.float32)
        * scaling
    )
    same_session = segment[:, :, None] == segment[:, None, :]
    scores = jnp.where(same_session[:, None], scores, -1e30)
    row_peak = jnp.max(scores, axis=-1, keepdims=True)
    exponent = jnp.exp(scores - row_peak)
    probabilities = exponent / jnp.sum(exponent, axis=-1, keepdims=True)
    prob_rounded = probabilities.astype(jnp.bfloat16)
    attended = rows_major(
        jnp.einsum(
            "bhqk,bhkd->bhqd", prob_rounded, value_rows, preferred_element_type=jnp.float32
        ).astype(jnp.bfloat16)
    )
    return queries, key_rows, value_rows, probabilities, prob_rounded, attended


def attention_backward(forward, upstream, weights_qkv, weights_out):
    queries, key_rows, value_rows, probabilities, prob_rounded, _ = forward
    blocks, heads = queries.shape[:2]
    scaling = HEAD_DIM ** (-0.5)
    grad_heads = jnp.einsum(
        "bqd,dhe->bhqe",
        upstream.reshape(blocks, upstream.shape[0] // blocks, upstream.shape[1]),
        weights_out.reshape(weights_out.shape[0], heads, HEAD_DIM),
        preferred_element_type=jnp.float32,
    ).astype(jnp.bfloat16)
    grad_prob = jnp.einsum(
        "bhqd,bhkd->bhqk", grad_heads, value_rows, preferred_element_type=jnp.float32
    )
    delta = jnp.sum(probabilities * grad_prob, axis=-1, keepdims=True)
    grad_score = lax.optimization_barrier(
        (probabilities * (grad_prob - delta) * scaling).astype(jnp.bfloat16)
    )
    grad_query = jnp.einsum(
        "bhqk,bhkd->bhqd", grad_score, key_rows, preferred_element_type=jnp.float32
    )
    grad_key = jnp.einsum(
        "bhqk,bhqd->bhkd", grad_score, queries, preferred_element_type=jnp.float32
    )
    grad_value = jnp.einsum(
        "bhqk,bhqd->bhkd", prob_rounded, grad_heads, preferred_element_type=jnp.float32
    )
    stacked = jnp.stack([grad_query, grad_key, grad_value]).astype(jnp.bfloat16)
    block_rows = stacked.shape[3]
    grad_normed = jnp.einsum(
        "sbhqe,dshe->bqd",
        stacked,
        weights_qkv.reshape(weights_qkv.shape[0], 3, heads, HEAD_DIM),
        preferred_element_type=jnp.float32,
    ).reshape(blocks * block_rows, weights_qkv.shape[0])
    return stacked, grad_normed


def embed_terms(embed_in_q, embed_out_q, aug_rows, grad_rows):
    pre = jnp.dot(embed_in_q.astype(jnp.float32), aug_rows, precision=lax.Precision.HIGHEST)
    hidden = gelu_value(pre).astype(jnp.bfloat16)
    term_out = jnp.dot(hidden, grad_rows, preferred_element_type=jnp.float32)
    grad_hidden = lax.dot_general(
        embed_out_q, grad_rows, (((1,), (1,)), ((), ())), preferred_element_type=jnp.float32
    )
    grad_pre = grad_hidden * gelu_slope(pre)
    term_in = lax.dot_general(
        grad_pre, aug_rows, (((1,), (1,)), ((), ())), precision=lax.Precision.HIGHEST
    )
    return (term_out, term_in)


def broadcast_from_first(block, axis):
    count = lax.axis_size(axis)
    index = lax.axis_index(axis)
    if count == 1:
        return block
    result = jnp.where(index == 0, block, lax.ppermute(block, axis, [(0, 1)]))
    if count > 2:
        back = lax.ppermute(block, axis, [(0, count - 1)])
        result = jnp.where(index == count - 1, back, result)
    if count <= 3:
        return result
    assert count == 4
    half = block.shape[0] // 2
    low = lax.ppermute(result[:half], axis, [(1, 2)])
    high = lax.ppermute(result[half:], axis, [(3, 2)])
    return jnp.where(index == 2, jnp.concatenate([low, high], axis=0), result)


def on_device(saved_inputs, attn_weights, grad_out, segments, coords, embed_in, embed_out):
    section_count = lax.axis_size("section")
    section_index = lax.axis_index("section")
    chip_count = lax.axis_size("xy")
    core = lax.axis_index("core")
    other = 1 - core
    micro_count = saved_inputs.shape[1]
    row_count = saved_inputs.shape[2]
    width = saved_inputs.shape[3]
    local_rows = attn_weights.shape[1]
    attn_width = attn_weights.shape[2] // 4
    half_width = attn_width // 2
    own_rows = micro_count * row_count
    embed_rows = embed_out.shape[0]

    mine = attn_weights[0].reshape(local_rows, 4, 2, half_width)
    given = swap_cores(pick(mine, other, 2))
    kept = pick(mine, core, 2)
    chip_rows = jnp.where(
        core == 0,
        jnp.concatenate([kept, given], axis=0),
        jnp.concatenate([given, kept], axis=0),
    ).reshape(2 * local_rows, 4 * half_width)
    layer = lax.all_gather(chip_rows, "xy", axis=0, tiled=True)
    weights_qkv = layer[:, : 3 * half_width]
    weights_out = layer[:, 3 * half_width :]

    embed_both = lax.all_gather(
        jnp.concatenate([embed_out, embed_in], axis=1), FSDP, axis=0, tiled=True
    )

    inputs_own = saved_inputs[0].reshape(own_rows, width)
    inputs_all = jnp.concatenate([inputs_own, swap_cores(inputs_own)], axis=0)
    segment_own = segments[:, 0, :]
    segment_all = jnp.concatenate([segment_own, swap_cores(segment_own)], axis=0)
    norm_scale_all, normed_all = normalize(inputs_all)
    norm_scale = norm_scale_all[:own_rows]
    values = inputs_own.astype(jnp.float32)
    forward = attention_forward(normed_all, weights_qkv, segment_all, 2 * micro_count)
    attended_all = forward[-1]

    top_grad = grad_out.reshape(own_rows, width)
    received = top_grad
    keep = None
    for step_index in range(section_count):
        active = section_count - 1 - step_index
        upstream = top_grad if step_index == 0 else received
        upstream_all = jnp.concatenate([upstream, swap_cores(upstream)], axis=0)
        grad_qkv, grad_normed = attention_backward(
            forward, upstream_all, weights_qkv, weights_out
        )
        grad_normed = grad_normed[:own_rows] + swap_cores(grad_normed[own_rows:])
        grad_inputs = (
            upstream.astype(jnp.float32)
            + norm_scale * grad_normed
            - values * norm_scale**3 * jnp.mean(values * grad_normed, axis=-1, keepdims=True)
        ).astype(jnp.bfloat16)
        fresh = (grad_qkv, upstream_all, grad_inputs)
        if keep is None:
            keep = fresh
        else:
            valid = section_index == active
            keep = tuple(jnp.where(valid, f, k) for f, k in zip(fresh, keep))
        if step_index < section_count - 1:
            pairs = [(i, i - 1) for i in range(1, section_count)]
            received = lax.ppermute(grad_inputs, "section", pairs)
    stacked_all, up_all, first_grad = keep
    qkv_all = stacked_all.transpose(1, 3, 0, 2, 4).reshape(
        up_all.shape[0], 3 * half_width
    )
    chip_tokens = qkv_all.shape[0]
    left = lax.optimization_barrier(jnp.concatenate([normed_all, up_all], axis=0).T)
    right = jnp.concatenate(
        [
            jnp.concatenate(
                [qkv_all, jnp.zeros((chip_tokens, half_width), qkv_all.dtype)], axis=1
            ),
            jnp.concatenate(
                [jnp.zeros((chip_tokens, 3 * half_width), qkv_all.dtype), attended_all], axis=1
            ),
        ],
        axis=0,
    )
    grad_half = jnp.dot(left, right, preferred_element_type=jnp.float32).astype(jnp.bfloat16)
    chip_grad = lax.psum_scatter(grad_half, "xy", scatter_dimension=0, tiled=True)
    chip_grad = chip_grad.reshape(2, local_rows, 4, half_width)
    mine_grad = pick(chip_grad, core, 0)
    theirs_grad = swap_cores(pick(chip_grad, other, 0))
    attn_grad = jnp.where(
        core == 0,
        jnp.stack([mine_grad, theirs_grad], axis=2),
        jnp.stack([theirs_grad, mine_grad], axis=2),
    ).reshape(local_rows, 4 * attn_width).astype(jnp.float32)

    input_grad = broadcast_from_first(first_grad, "section")
    grad_all = jnp.concatenate([input_grad, swap_cores(input_grad)], axis=0)
    coords_own = coords.reshape(3, own_rows)
    coords_all = jnp.concatenate([coords_own, swap_cores(coords_own)], axis=1)
    augmented = jnp.concatenate(
        [coords_all, jnp.ones((1, 2 * own_rows), jnp.float32)], axis=0
    )
    embed_half = pick(
        embed_both.reshape(chip_count, 2, embed_rows, width + embed_in.shape[1]), core, 1
    ).reshape(chip_count * embed_rows, width + embed_in.shape[1])
    term_out, term_in = embed_terms(
        embed_half[:, width:], embed_half[:, :width], augmented, grad_all
    )
    terms = jnp.concatenate([term_out, term_in], axis=1).astype(jnp.bfloat16)
    pieces = lax.all_to_all(
        terms.reshape(chip_count, embed_rows, terms.shape[1]), "xy", 0, 0, tiled=False
    )
    summed = jnp.sum(pieces.astype(jnp.float32), axis=0)
    return (
        attn_grad[None],
        input_grad.reshape(micro_count, row_count, width),
        summed[:, :width],
        summed[:, width:],
    )


def solution(mesh):
    sections, fsdp = mesh.devices.shape
    inner = Mesh(mesh.devices.reshape(sections, fsdp // 2, 2), ("section", "xy", "core"))
    placed = (
        P("section", None, FSDP, None),
        P("section", FSDP, None),
        P(None, FSDP, None),
        P(None, FSDP, None),
        P(None, None, FSDP),
        P(("section",) + FSDP, None),
        P(("section",) + FSDP, None),
    )
    outer_specs = (
        P("section", "fsdp", None),
        P(None, "fsdp", None),
        P(("section", "fsdp"), None),
        P(("section", "fsdp"), None),
    )
    mapped = jax.shard_map(
        on_device,
        mesh=inner,
        in_specs=placed,
        out_specs=(
            P("section", FSDP, None),
            P(None, FSDP, None),
            P(("section",) + FSDP, None),
            P(("section",) + FSDP, None),
        ),
        check_vma=False,
    )

    def run(*args):
        outs = mapped(*args)
        return tuple(
            lax.with_sharding_constraint(o, NamedSharding(mesh, s))
            for o, s in zip(outs, outer_specs)
        )

    return run
```

```python
import jax
import jax.numpy as jnp
from jax import lax
from jax.sharding import Mesh, NamedSharding, PartitionSpec as P

HEAD_DIM = 64


EPS = 1e-05

FSDP = ("xy", "core")


def gelu_value(pre):
    return 0.5 * pre * (1.0 + jax.scipy.special.erf(pre / jnp.sqrt(2.0)))


def gelu_slope(pre):
    return 0.5 * (1.0 + jax.scipy.special.erf(pre / jnp.sqrt(2.0))) + pre * jnp.exp(
        -0.5 * pre * pre
    ) / jnp.sqrt(2.0 * jnp.pi)


def normalize(inputs):
    values = inputs.astype(jnp.float32)
    norm_scale = lax.rsqrt(jnp.mean(values * values, axis=-1, keepdims=True) + EPS)
    normed = (values * norm_scale).astype(jnp.bfloat16)
    return (norm_scale, normed)


def swap_cores(value):
    return lax.ppermute(value, "core", [(0, 1), (1, 0)])


def pick(value, index, axis):
    return lax.dynamic_index_in_dim(value, index, axis, keepdims=False)


def heads_major(rows, blocks, heads):
    return rows.reshape(blocks, rows.shape[0] // blocks, heads, HEAD_DIM).transpose(0, 2, 1, 3)


def rows_major(value):
    blocks, heads, block_rows, _ = value.shape
    return value.transpose(0, 2, 1, 3).reshape(blocks * block_rows, heads * HEAD_DIM)


def attention_forward(normed, weights_qkv, segment, blocks):
    width = weights_qkv.shape[1] // 3
    heads = width // HEAD_DIM
    scaling = HEAD_DIM ** (-0.5)
    projected = jnp.dot(
        normed, weights_qkv, preferred_element_type=jnp.float32
    ).astype(jnp.bfloat16)
    queries = heads_major(projected[:, :width], blocks, heads)
    key_rows = heads_major(projected[:, width : 2 * width], blocks, heads)
    value_rows = heads_major(projected[:, 2 * width :], blocks, heads)
    scores = (
        jnp.einsum("bhqd,bhkd->bhqk", queries, key_rows, preferred_element_type=jnp.float32)
        * scaling
    )
    same_session = segment[:, :, None] == segment[:, None, :]
    scores = jnp.where(same_session[:, None], scores, -1e30)
    row_peak = jnp.max(scores, axis=-1, keepdims=True)
    exponent = jnp.exp(scores - row_peak)
    probabilities = exponent / jnp.sum(exponent, axis=-1, keepdims=True)
    prob_rounded = probabilities.astype(jnp.bfloat16)
    attended = rows_major(
        jnp.einsum(
            "bhqk,bhkd->bhqd", prob_rounded, value_rows, preferred_element_type=jnp.float32
        ).astype(jnp.bfloat16)
    )
    return queries, key_rows, value_rows, probabilities, prob_rounded, attended


def attention_backward(forward, upstream, weights_qkv, weights_out):
    queries, key_rows, value_rows, probabilities, prob_rounded, _ = forward
    blocks, heads = queries.shape[:2]
    scaling = HEAD_DIM ** (-0.5)
    grad_heads = jnp.einsum(
        "bqd,dhe->bhqe",
        upstream.reshape(blocks, upstream.shape[0] // blocks, upstream.shape[1]),
        weights_out.reshape(weights_out.shape[0], heads, HEAD_DIM),
        preferred_element_type=jnp.float32,
    ).astype(jnp.bfloat16)
    grad_prob = jnp.einsum(
        "bhqd,bhkd->bhqk", grad_heads, value_rows, preferred_element_type=jnp.float32
    )
    delta = jnp.sum(probabilities * grad_prob, axis=-1, keepdims=True)
    grad_score = lax.optimization_barrier(
        (probabilities * (grad_prob - delta) * scaling).astype(jnp.bfloat16)
    )
    grad_query = jnp.einsum(
        "bhqk,bhkd->bhqd", grad_score, key_rows, preferred_element_type=jnp.float32
    )
    grad_key = jnp.einsum(
        "bhqk,bhqd->bhkd", grad_score, queries, preferred_element_type=jnp.float32
    )
    grad_value = jnp.einsum(
        "bhqk,bhqd->bhkd", prob_rounded, grad_heads, preferred_element_type=jnp.float32
    )
    stacked = jnp.stack([grad_query, grad_key, grad_value]).astype(jnp.bfloat16)
    block_rows = stacked.shape[3]
    grad_normed = jnp.einsum(
        "sbhqe,dshe->bqd",
        stacked,
        weights_qkv.reshape(weights_qkv.shape[0], 3, heads, HEAD_DIM),
        preferred_element_type=jnp.float32,
    ).reshape(blocks * block_rows, weights_qkv.shape[0])
    return stacked, grad_normed


def embed_terms(embed_in_q, embed_out_q, aug_rows, grad_rows):
    pre = jnp.dot(embed_in_q.astype(jnp.float32), aug_rows, precision=lax.Precision.HIGHEST)
    hidden = gelu_value(pre).astype(jnp.bfloat16)
    term_out = jnp.dot(hidden, grad_rows, preferred_element_type=jnp.float32)
    grad_hidden = lax.dot_general(
        embed_out_q, grad_rows, (((1,), (1,)), ((), ())), preferred_element_type=jnp.float32
    )
    grad_pre = grad_hidden * gelu_slope(pre)
    term_in = lax.dot_general(
        grad_pre, aug_rows, (((1,), (1,)), ((), ())), precision=lax.Precision.HIGHEST
    )
    return (term_out, term_in)


def broadcast_from_first(block, axis):
    count = lax.axis_size(axis)
    index = lax.axis_index(axis)
    if count == 1:
        return block
    result = jnp.where(index == 0, block, lax.ppermute(block, axis, [(0, 1)]))
    if count > 2:
        back = lax.ppermute(block, axis, [(0, count - 1)])
        result = jnp.where(index == count - 1, back, result)
    if count <= 3:
        return result
    assert count == 4
    half = block.shape[0] // 2
    low = lax.ppermute(result[:half], axis, [(1, 2)])
    high = lax.ppermute(result[half:], axis, [(3, 2)])
    return jnp.where(index == 2, jnp.concatenate([low, high], axis=0), result)


def on_device(saved_inputs, attn_weights, grad_out, segments, coords, embed_in, embed_out):
    section_count = lax.axis_size("section")
    section_index = lax.axis_index("section")
    chip_count = lax.axis_size("xy")
    core = lax.axis_index("core")
    other = 1 - core
    micro_count = saved_inputs.shape[1]
    row_count = saved_inputs.shape[2]
    width = saved_inputs.shape[3]
    local_rows = attn_weights.shape[1]
    attn_width = attn_weights.shape[2] // 4
    half_width = attn_width // 2
    own_rows = micro_count * row_count
    embed_rows = embed_out.shape[0]

    mine = attn_weights[0].reshape(local_rows, 4, 2, half_width)
    given = swap_cores(jnp.where(core == 0, mine[:, :, 1], mine[:, :, 0]))
    kept = jnp.where(core == 0, mine[:, :, 0], mine[:, :, 1])
    chip_rows = jnp.where(
        core == 0,
        jnp.concatenate([kept, given], axis=0),
        jnp.concatenate([given, kept], axis=0),
    ).reshape(2 * local_rows, 4 * half_width)
    layer = lax.all_gather(chip_rows, "xy", axis=0, tiled=True)
    weights_qkv = layer[:, : 3 * half_width]
    weights_out = layer[:, 3 * half_width :]

    embed_both = lax.all_gather(
        jnp.concatenate([embed_out, embed_in], axis=1), FSDP, axis=0, tiled=True
    )

    inputs_own = saved_inputs[0].reshape(own_rows, width)
    inputs_all = jnp.concatenate([inputs_own, swap_cores(inputs_own)], axis=0)
    segment_own = segments[:, 0, :]
    segment_all = jnp.concatenate([segment_own, swap_cores(segment_own)], axis=0)
    norm_scale_all, normed_all = normalize(inputs_all)
    norm_scale = norm_scale_all[:own_rows]
    values = inputs_own.astype(jnp.float32)
    forward = attention_forward(normed_all, weights_qkv, segment_all, 2 * micro_count)
    attended_all = forward[-1]

    top_grad = grad_out.reshape(own_rows, width)
    received = top_grad
    keep = None
    for step_index in range(section_count):
        active = section_count - 1 - step_index
        upstream = top_grad if step_index == 0 else received
        upstream_all = jnp.concatenate([upstream, swap_cores(upstream)], axis=0)
        grad_qkv, grad_normed = attention_backward(
            forward, upstream_all, weights_qkv, weights_out
        )
        grad_normed = grad_normed[:own_rows] + swap_cores(grad_normed[own_rows:])
        grad_inputs = (
            upstream.astype(jnp.float32)
            + norm_scale * grad_normed
            - values * norm_scale**3 * jnp.mean(values * grad_normed, axis=-1, keepdims=True)
        ).astype(jnp.bfloat16)
        fresh = (grad_qkv, upstream_all, grad_inputs)
        if keep is None:
            keep = fresh
        else:
            valid = section_index == active
            keep = tuple(jnp.where(valid, f, k) for f, k in zip(fresh, keep))
        if step_index < section_count - 1:
            pairs = [(i, i - 1) for i in range(1, section_count)]
            received = lax.ppermute(grad_inputs, "section", pairs)
    stacked_all, up_all, first_grad = keep
    qkv_all = stacked_all.transpose(1, 3, 0, 2, 4).reshape(
        up_all.shape[0], 3 * half_width
    )
    chip_tokens = qkv_all.shape[0]
    left = lax.optimization_barrier(jnp.concatenate([normed_all, up_all], axis=0).T)
    right = jnp.concatenate(
        [
            jnp.concatenate(
                [qkv_all, jnp.zeros((chip_tokens, half_width), qkv_all.dtype)], axis=1
            ),
            jnp.concatenate(
                [jnp.zeros((chip_tokens, 3 * half_width), qkv_all.dtype), attended_all], axis=1
            ),
        ],
        axis=0,
    )
    grad_half = jnp.dot(left, right, preferred_element_type=jnp.float32).astype(jnp.bfloat16)
    chip_grad = lax.psum_scatter(grad_half, "xy", scatter_dimension=0, tiled=True)
    chip_grad = chip_grad.reshape(2, local_rows, 4, half_width)
    mine_grad = pick(chip_grad, core, 0)
    theirs_grad = swap_cores(pick(chip_grad, other, 0))
    attn_grad = jnp.where(
        core == 0,
        jnp.stack([mine_grad, theirs_grad], axis=2),
        jnp.stack([theirs_grad, mine_grad], axis=2),
    ).reshape(local_rows, 4 * attn_width).astype(jnp.float32)

    input_grad = broadcast_from_first(first_grad, "section")
    grad_all = jnp.concatenate([input_grad, swap_cores(input_grad)], axis=0)
    coords_own = coords.reshape(3, own_rows)
    coords_all = jnp.concatenate([coords_own, swap_cores(coords_own)], axis=1)
    augmented = jnp.concatenate(
        [coords_all, jnp.ones((1, 2 * own_rows), jnp.float32)], axis=0
    )
    embed_half = pick(
        embed_both.reshape(chip_count, 2, embed_rows, width + embed_in.shape[1]), core, 1
    ).reshape(chip_count * embed_rows, width + embed_in.shape[1])
    term_out, term_in = embed_terms(
        embed_half[:, width:], embed_half[:, :width], augmented, grad_all
    )
    terms = jnp.concatenate([term_out, term_in], axis=1).astype(jnp.bfloat16)
    pieces = lax.all_to_all(
        terms.reshape(chip_count, embed_rows, terms.shape[1]), "xy", 0, 0, tiled=False
    )
    summed = jnp.sum(pieces.astype(jnp.float32), axis=0)
    return (
        attn_grad[None],
        input_grad.reshape(micro_count, row_count, width),
        summed[:, :width],
        summed[:, width:],
    )


def solution(mesh):
    sections, fsdp = mesh.devices.shape
    inner = Mesh(mesh.devices.reshape(sections, fsdp // 2, 2), ("section", "xy", "core"))
    placed = (
        P("section", None, FSDP, None),
        P("section", FSDP, None),
        P(None, FSDP, None),
        P(None, FSDP, None),
        P(None, None, FSDP),
        P(("section",) + FSDP, None),
        P(("section",) + FSDP, None),
    )
    outer_specs = (
        P("section", "fsdp", None),
        P(None, "fsdp", None),
        P(("section", "fsdp"), None),
        P(("section", "fsdp"), None),
    )
    mapped = jax.shard_map(
        on_device,
        mesh=inner,
        in_specs=placed,
        out_specs=(
            P("section", FSDP, None),
            P(None, FSDP, None),
            P(("section",) + FSDP, None),
            P(("section",) + FSDP, None),
        ),
        check_vma=False,
    )

    def run(*args):
        outs = mapped(*args)
        return tuple(
            lax.with_sharding_constraint(o, NamedSharding(mesh, s))
            for o, s in zip(outs, outer_specs)
        )

    return run
```
